32 devices in a mesh: task: 2 (over y), row: 4 (over z), col: 4 (over x, core).
Axes of the slice: x: 2, y: 2, z: 4, core: 2. Of those that a mesh axis runs over, the one named last changes fastest.
Arguments:
- features: bfloat16 [164, 4096], P(None, ('task', 'row', 'col')), parts along dimension 1, may hold values from -6 to 6
- rung_index: int32 [4096], P(('task', 'row', 'col')), parts along dimension 0, may hold values from 0 to 3
- w_first: bfloat16 [164, 512], replicated, may hold values from -0.5 to 0.5
- b_first: float32 [512], replicated, may hold values from -4 to 4
- w_second: bfloat16 [512, 512], replicated, may hold values from -0.25 to 0.25
- b_second: float32 [512], replicated, may hold values from -4 to 4
- w_third: bfloat16 [512, 64], replicated, may hold values from -0.25 to 0.25
- targets: float32 [16, 4096], P(None, ('task', 'row', 'col')), parts along dimension 1, may hold values from -80 to 80
- fidelity_factor: float32 [8, 4], P('task'), parts along dimension 0, may hold values from -4 to 4
- inverse_scale: float32 [2], P('task'), parts along dimension 0, may hold values from 0.02 to 0.1
- noise_var: float32 [2], P('task'), parts along dimension 0, may hold values from 0.3 to 1
Outputs:
- solution: float32 [16, 4096], P(None, ('task', 'row', 'col')), parts along dimension 1
- residual: float32 [16, 4096], P(None, ('task', 'row', 'col')), parts along dimension 1
The draws below stay inside these ranges and needn't reach their ends.
There are 2 independent parts, one for each index of `task`. The reference program is written for one: setup_inputs(seed, part) draws one part's arguments, and reference() takes and returns one part's arrays. A program takes and returns all parts, laid end to end along the dimension named above; an argument that names none is the same for every part. Nothing has to cross between parts.
All inputs are finite; a program needn't handle non-finite values.
Results may differ from the reference program's by a relative error of at most 0.012.
The reference program's roundings to bfloat16 on the way (of `hidden_one`, `hidden_two` and `embedding`) count: a program that leaves them out, or rounds other values in their place, can miss the bound.
Values may be sent and summed in bfloat16 or wider, within the bound.
No kernel may reach another device: no remote copies, remote signals or barrier semaphores. Data moves between devices by JAX's collectives and lax.ppermute only.
A program may use at most 64 MiB of HBM per device.

```python
import math
import jax
import jax.numpy as jnp
from jax import lax

FEAT = 164
HIDDEN_UNITS = 512
EMB = 64
RUNGS = 4
RHS = 16
ITERS = 2
PLANS = 2048


def draw_targets(key, part):
    first_key, second_key, third_key = jax.random.split(jax.random.fold_in(key, 17), 3)
    position = jnp.arange(PLANS, dtype=jnp.float32) / float(PLANS)
    rising = 1.0 + 2.0 * position
    column_scale = 0.5 * jnp.exp(jax.random.uniform(second_key, (1, PLANS), jnp.float32) * math.log(3.3))
    side_scale = 0.3 * jnp.exp(jax.random.uniform(third_key, (RHS, 1), jnp.float32) * math.log(10.0))
    values = jnp.clip(jax.random.normal(first_key, (RHS, PLANS), jnp.float32), -5.0, 5.0)
    return (values * side_scale * column_scale * rising[None, :]).astype(jnp.float32)


def with_ends(array, key, smallest, high):
    shape = array.shape
    index_at = [jax.random.randint(jax.random.fold_in(key, axis), (), 0, shape[axis]) for axis in range(len(shape))]
    array = array.at[tuple(index_at)].set(smallest)
    longest = shape.index(max(shape))
    index_at[longest] = (index_at[longest] + 1) % shape[longest]
    return array.at[tuple(index_at)].set(high)


def level_of(key, dims, cuts, low, high):
    level = 1.0
    for axis_at, blocks in cuts:
        steps = jax.random.uniform(jax.random.fold_in(jax.random.fold_in(key, 6), axis_at), (blocks,), jnp.float32, low / len(cuts), high / len(cuts))
        level = level * jnp.repeat(jnp.exp(steps), dims[axis_at] // blocks).reshape((-1,) + (1,) * (len(dims) - 1 - axis_at))
    return level


def gaussian(own_key, dims, scale, limit, cuts=(), held_as=jnp.bfloat16):
    drawn = jax.random.normal(own_key, dims, jnp.float32) * scale
    if len(cuts) > 0:
        drawn = level_of(own_key, dims, cuts, -0.22, 0.18) * drawn
    return jnp.clip(drawn, min=-limit, max=limit).astype(held_as)


def setup_inputs(seed: int = 0, part: int = 0) -> dict:
    splits = jax.random.split(jax.random.key(seed), 12)
    part_keys = jax.random.split(jax.random.fold_in(splits[11], part), 12)
    features = gaussian(part_keys[0], (FEAT, PLANS), 1.0, 6.0, ((1, 16),))
    rung_index = with_ends(jax.random.randint(part_keys[1], (PLANS,), 0, RUNGS), jax.random.fold_in(part_keys[1], 1), 0, RUNGS - 1).astype(jnp.int32)
    w_first = gaussian(splits[2], (FEAT, HIDDEN_UNITS), FEAT ** -0.5, 0.5)
    b_first = gaussian(splits[3], (HIDDEN_UNITS,), 1.0, 4.0, (), jnp.float32)
    w_second = gaussian(splits[4], (HIDDEN_UNITS, HIDDEN_UNITS), HIDDEN_UNITS ** -0.5, 0.25)
    b_second = gaussian(splits[5], (HIDDEN_UNITS,), 1.0, 4.0, (), jnp.float32)
    w_third = gaussian(splits[6], (HIDDEN_UNITS, EMB), HIDDEN_UNITS ** -0.5, 0.25)
    targets = draw_targets(jax.random.fold_in(jax.random.fold_in(splits[11], part), 71), part)
    fidelity_factor = gaussian(part_keys[8], (RUNGS, RUNGS), 0.7, 4.0, (), jnp.float32)
    inverse_scale = jnp.clip(jnp.exp(jax.random.uniform(part_keys[9], (1,), jnp.float32, math.log(0.02), math.log(0.1))), 0.02, 0.1)
    noise_var = jnp.clip(jnp.exp(jax.random.uniform(part_keys[10], (1,), jnp.float32, math.log(0.3), math.log(1.0))), 0.3, 1.0)
    return {"features": features, "rung_index": rung_index, "w_first": w_first, "b_first": b_first, "w_second": w_second, "b_second": b_second, "w_third": w_third, "targets": targets, "fidelity_factor": fidelity_factor, "inverse_scale": inverse_scale, "noise_var": noise_var}


def fidelity_matrix(fidelity_factor):
    lower = jnp.tril(fidelity_factor)
    return jnp.dot(lower, lower.T, precision=lax.Precision.HIGHEST) + 0.5 * jnp.eye(fidelity_factor.shape[0], dtype=jnp.float32)

def left_product(weights, values):
    return lax.dot_general(weights.astype(jnp.float32), values.astype(jnp.float32), (((0,), (0,)), ((), ())), preferred_element_type=jnp.float32)

def embed_all(features, w_first, b_first, w_second, b_second, w_third):
    hidden_one = jax.nn.silu(left_product(w_first, features) + b_first[:, None]).astype(jnp.bfloat16)
    hidden_two = jax.nn.silu(left_product(w_second, hidden_one) + b_second[:, None]).astype(jnp.bfloat16)
    return left_product(w_third, hidden_two).astype(jnp.bfloat16)

def kernel_product(embedding, rung_index, fidelity, inverse_scale, direction):
    total_rows = embedding.shape[1]
    block_rows = math.gcd(total_rows, 1024)
    squares = jnp.sum(jnp.square(embedding.astype(jnp.float32)), axis=0)

    def one_block(block_number):
        first_row = (block_number * block_rows).astype(jnp.int32)
        rows_embedding = lax.dynamic_slice_in_dim(embedding, first_row, block_rows, 1)
        rows_squares = lax.dynamic_slice_in_dim(squares, first_row, block_rows, 0)
        rows_rung = lax.dynamic_slice_in_dim(rung_index, first_row, block_rows, 0)
        inner = left_product(rows_embedding, embedding)
        distance = rows_squares[:, None] + squares[None, :] - 2.0 * inner
        kernel = jnp.exp(-inverse_scale[0] * distance) * fidelity[rows_rung[:, None], rung_index[None, :]]
        return lax.dot_general(direction, kernel, (((1,), (1,)), ((), ())), precision=lax.Precision.HIGHEST)
    stacked = lax.map(one_block, jnp.arange(total_rows // block_rows, dtype=jnp.int32))
    return jnp.transpose(stacked, (1, 0, 2)).reshape(direction.shape[0], total_rows)

def outer_gram(left_side, right_side):
    return lax.dot_general(left_side, right_side, (((1,), (1,)), ((), ())), precision=lax.Precision.HIGHEST)

def solve_spd(matrix, right_side):
    return jax.scipy.linalg.cho_solve((jnp.linalg.cholesky(matrix), True), right_side)

def reference(features, rung_index, w_first, b_first, w_second, b_second, w_third, targets, fidelity_factor, inverse_scale, noise_var):
    fidelity = fidelity_matrix(fidelity_factor)
    embedding = embed_all(features, w_first, b_first, w_second, b_second, w_third)
    solution = jnp.zeros_like(targets)
    residual = targets
    direction = targets
    gram = outer_gram(residual, residual)
    for iteration in range(ITERS):
        image = kernel_product(embedding, rung_index, fidelity, inverse_scale, direction) + noise_var[0] * direction
        curvature = outer_gram(direction, image)
        step_matrix = solve_spd(curvature, gram)
        solution = solution + jnp.dot(step_matrix.T, direction, precision=lax.Precision.HIGHEST)
        residual = residual - jnp.dot(step_matrix.T, image, precision=lax.Precision.HIGHEST)
        if iteration + 1 < ITERS:
            new_gram = outer_gram(residual, residual)
            update_matrix = solve_spd(gram, new_gram)
            direction = residual + jnp.dot(update_matrix.T, direction, precision=lax.Precision.HIGHEST)
            gram = new_gram
    return (solution, residual)
```

```python
import jax
import jax.numpy as jnp
from jax import lax
from jax.sharding import PartitionSpec as P

ITERS = 2


def fidelity_matrix(fidelity_factor):
    lower = jnp.tril(fidelity_factor)
    return jnp.dot(lower, lower.T, precision=lax.Precision.HIGHEST) + 0.5 * jnp.eye(
        fidelity_factor.shape[0], dtype=jnp.float32
    )


def left_product(weights, values):
    return lax.dot_general(
        weights, values, (((0,), (0,)), ((), ())), preferred_element_type=jnp.float32
    )


def outer_gram(left_side, right_side):
    return lax.dot_general(
        left_side, right_side, (((1,), (1,)), ((), ())), precision=lax.Precision.HIGHEST
    )


def solve_spd(matrix, right_side):
    return jax.scipy.linalg.cho_solve((jnp.linalg.cholesky(matrix), True), right_side)


def block_size(total_count, largest):
    chosen = min(total_count, largest)
    while total_count % chosen != 0:
        chosen = chosen - 1
    return chosen


def rung_fidelity(fidelity, rung_value):
    levels = jnp.arange(fidelity.shape[0], dtype=jnp.float32)
    onehot = (rung_value.astype(jnp.float32)[None, :] == levels[:, None]).astype(jnp.float32)
    return jnp.dot(fidelity, onehot, precision=lax.Precision.HIGHEST)


def kernel_image(embedding, squares, rung_value, col_fidelity, inverse_scale, direction):
    count = embedding.shape[1]
    row_block = block_size(count, 2048)
    col_block = block_size(count, 2048)
    levels = jnp.arange(col_fidelity.shape[0], dtype=jnp.float32)

    def one_row_block(block_number):
        first_row = block_number * row_block
        rows_embedding = lax.dynamic_slice_in_dim(embedding, first_row, row_block, 1)
        rows_squares = lax.dynamic_slice_in_dim(squares, first_row, row_block, 0)
        rows_rung = lax.dynamic_slice_in_dim(rung_value, first_row, row_block, 0)
        rows_match = rows_rung.astype(jnp.float32)[:, None] == levels[None, :]

        def one_col_block(running, column_number):
            first_col = column_number * col_block
            cols_embedding = lax.dynamic_slice_in_dim(embedding, first_col, col_block, 1)
            cols_squares = lax.dynamic_slice_in_dim(squares, first_col, col_block, 0)
            cols_fidelity = lax.dynamic_slice_in_dim(col_fidelity, first_col, col_block, 1)
            cols_direction = lax.dynamic_slice_in_dim(direction, first_col, col_block, 1)
            inner = left_product(rows_embedding, cols_embedding)
            distance = rows_squares[:, None] + cols_squares[None, :] - 2.0 * inner
            tile_fidelity = cols_fidelity[0][None, :]
            for level in range(1, col_fidelity.shape[0]):
                tile_fidelity = jnp.where(
                    rows_match[:, level : level + 1], cols_fidelity[level][None, :], tile_fidelity
                )
            kernel = jnp.exp(-inverse_scale[0] * distance) * tile_fidelity
            contribution = lax.dot_general(
                cols_direction, kernel, (((1,), (1,)), ((), ())), precision=lax.Precision.HIGHEST
            )
            return (running + contribution, None)

        start_value = jnp.zeros((direction.shape[0], row_block), jnp.float32)
        result, unused = lax.scan(
            one_col_block, start_value, jnp.arange(count // col_block, dtype=jnp.int32)
        )
        return result

    stacked = lax.map(one_row_block, jnp.arange(count // row_block, dtype=jnp.int32))
    return jnp.transpose(stacked, (1, 0, 2)).reshape(direction.shape[0], count)


def on_device(
    features,
    rung_index,
    w_first,
    b_first,
    w_second,
    b_second,
    w_third,
    targets,
    fidelity_factor,
    inverse_scale,
    noise_var,
):
    fidelity = fidelity_matrix(fidelity_factor)
    hidden_one = jax.nn.silu(left_product(w_first, features) + b_first[:, None]).astype(
        jnp.bfloat16
    )
    hidden_two = jax.nn.silu(left_product(w_second, hidden_one) + b_second[:, None]).astype(
        jnp.bfloat16
    )
    embedding = left_product(w_third, hidden_two).astype(jnp.bfloat16)
    rung_value = rung_index.astype(jnp.float32).astype(jnp.bfloat16)
    own_count = targets.shape[1]
    own_first = (lax.axis_index("row") * lax.axis_size("col") + lax.axis_index("col")) * own_count

    all_embedding = lax.all_gather(embedding, ("row", "col"), axis=1, tiled=True)
    all_rung = lax.all_gather(rung_value, ("row", "col"), axis=0, tiled=True)
    all_targets = lax.all_gather(targets, ("row", "col"), axis=1, tiled=True)

    squares = jnp.sum(jnp.square(all_embedding.astype(jnp.float32)), axis=0)
    col_fidelity = rung_fidelity(fidelity, all_rung)

    solution = jnp.zeros_like(all_targets)
    residual = all_targets
    direction = all_targets
    gram = outer_gram(residual, residual)
    for iteration in range(ITERS):
        image = (
            kernel_image(all_embedding, squares, all_rung, col_fidelity, inverse_scale, direction)
            + noise_var[0] * direction
        )
        curvature = outer_gram(direction, image)
        step_matrix = solve_spd(curvature, gram)
        solution = solution + jnp.dot(step_matrix.T, direction, precision=lax.Precision.HIGHEST)
        residual = residual - jnp.dot(step_matrix.T, image, precision=lax.Precision.HIGHEST)
        if iteration + 1 < ITERS:
            new_gram = outer_gram(residual, residual)
            update_matrix = solve_spd(gram, new_gram)
            direction = residual + jnp.dot(
                update_matrix.T, direction, precision=lax.Precision.HIGHEST
            )
            gram = new_gram
    own_solution = lax.dynamic_slice_in_dim(solution, own_first, own_count, 1)
    own_residual = lax.dynamic_slice_in_dim(residual, own_first, own_count, 1)
    return (own_solution, own_residual)


def solution(mesh):
    placed = (
        P(None, ("task", "row", "col")),
        P(("task", "row", "col")),
        P(),
        P(),
        P(),
        P(),
        P(),
        P(None, ("task", "row", "col")),
        P("task", None),
        P("task"),
        P("task"),
    )
    return jax.shard_map(
        on_device,
        mesh=mesh,
        in_specs=placed,
        out_specs=(P(None, ("task", "row", "col")), P(None, ("task", "row", "col"))),
        check_vma=False,
    )
```

```python
import jax
import jax.numpy as jnp
from jax import lax
from jax.sharding import PartitionSpec as P

ITERS = 2


def fidelity_matrix(fidelity_factor):
    lower = jnp.tril(fidelity_factor)
    return jnp.dot(lower, lower.T, precision=lax.Precision.HIGHEST) + 0.5 * jnp.eye(
        fidelity_factor.shape[0], dtype=jnp.float32
    )


def left_product(weights, values):
    return lax.dot_general(
        weights, values, (((0,), (0,)), ((), ())), preferred_element_type=jnp.float32
    )


def outer_gram(left_side, right_side):
    return lax.dot_general(
        left_side, right_side, (((1,), (1,)), ((), ())), precision=lax.Precision.HIGHEST
    )


def solve_spd(matrix, right_side):
    return jax.scipy.linalg.cho_solve((jnp.linalg.cholesky(matrix), True), right_side)


def block_size(total_count, largest):
    chosen = min(total_count, largest)
    while total_count % chosen != 0:
        chosen = chosen - 1
    return chosen


def rung_fidelity(fidelity, rung_value):
    levels = jnp.arange(fidelity.shape[0], dtype=jnp.float32)
    onehot = (rung_value.astype(jnp.float32)[None, :] == levels[:, None]).astype(jnp.float32)
    return jnp.dot(fidelity, onehot, precision=lax.Precision.HIGHEST)


def kernel_image(embedding, squares, rung_value, col_fidelity, inverse_scale, direction):
    count = embedding.shape[1]
    row_block = block_size(count, 2048)
    col_block = block_size(count, 2048)
    levels = jnp.arange(col_fidelity.shape[0], dtype=jnp.float32)

    def one_row_block(block_number):
        first_row = block_number * row_block
        rows_embedding = lax.dynamic_slice_in_dim(embedding, first_row, row_block, 1)
        rows_squares = lax.dynamic_slice_in_dim(squares, first_row, row_block, 0)
        rows_rung = lax.dynamic_slice_in_dim(rung_value, first_row, row_block, 0)
        rows_match = rows_rung.astype(jnp.float32)[:, None] == levels[None, :]

        def one_col_block(running, column_number):
            first_col = column_number * col_block
            cols_embedding = lax.dynamic_slice_in_dim(embedding, first_col, col_block, 1)
            cols_squares = lax.dynamic_slice_in_dim(squares, first_col, col_block, 0)
            cols_fidelity = lax.dynamic_slice_in_dim(col_fidelity, first_col, col_block, 1)
            cols_direction = lax.dynamic_slice_in_dim(direction, first_col, col_block, 1)
            inner = left_product(rows_embedding, cols_embedding)
            distance = rows_squares[:, None] + cols_squares[None, :] - 2.0 * inner
            tile_fidelity = cols_fidelity[0][None, :]
            for level in range(1, col_fidelity.shape[0]):
                tile_fidelity = jnp.where(
                    rows_match[:, level : level + 1], cols_fidelity[level][None, :], tile_fidelity
                )
            kernel = jnp.exp(-inverse_scale[0] * distance) * tile_fidelity
            contribution = lax.dot_general(
                cols_direction, kernel, (((1,), (1,)), ((), ())), precision=lax.Precision.HIGH
            )
            return (running + contribution, None)

        start_value = jnp.zeros((direction.shape[0], row_block), jnp.float32)
        result, unused = lax.scan(
            one_col_block, start_value, jnp.arange(count // col_block, dtype=jnp.int32)
        )
        return result

    stacked = lax.map(one_row_block, jnp.arange(count // row_block, dtype=jnp.int32))
    return jnp.transpose(stacked, (1, 0, 2)).reshape(direction.shape[0], count)


def on_device(
    features,
    rung_index,
    w_first,
    b_first,
    w_second,
    b_second,
    w_third,
    targets,
    fidelity_factor,
    inverse_scale,
    noise_var,
):
    fidelity = fidelity_matrix(fidelity_factor)
    hidden_one = jax.nn.silu(left_product(w_first, features) + b_first[:, None]).astype(
        jnp.bfloat16
    )
    hidden_two = jax.nn.silu(left_product(w_second, hidden_one) + b_second[:, None]).astype(
        jnp.bfloat16
    )
    embedding = left_product(w_third, hidden_two).astype(jnp.bfloat16)
    rung_value = rung_index.astype(jnp.float32).astype(jnp.bfloat16)
    own_count = targets.shape[1]
    own_first = (lax.axis_index("row") * lax.axis_size("col") + lax.axis_index("col")) * own_count

    emb_rows = embedding.shape[0]
    packed = jnp.concatenate(
        [embedding.astype(jnp.float32), targets, rung_value.astype(jnp.float32)[None, :]], axis=0
    )
    gathered = lax.all_gather(packed, ("row", "col"), axis=1, tiled=True)
    all_embedding = gathered[:emb_rows].astype(jnp.bfloat16)
    all_targets = gathered[emb_rows : emb_rows + targets.shape[0]]
    all_rung = gathered[emb_rows + targets.shape[0]]

    squares = jnp.sum(jnp.square(all_embedding.astype(jnp.float32)), axis=0)
    col_fidelity = rung_fidelity(fidelity, all_rung)

    solution = jnp.zeros_like(all_targets)
    residual = all_targets
    direction = all_targets
    gram = outer_gram(residual, residual)
    for iteration in range(ITERS):
        image = (
            kernel_image(all_embedding, squares, all_rung, col_fidelity, inverse_scale, direction)
            + noise_var[0] * direction
        )
        curvature = outer_gram(direction, image)
        step_matrix = solve_spd(curvature, gram)
        solution = solution + jnp.dot(step_matrix.T, direction, precision=lax.Precision.HIGHEST)
        residual = residual - jnp.dot(step_matrix.T, image, precision=lax.Precision.HIGHEST)
        if iteration + 1 < ITERS:
            new_gram = outer_gram(residual, residual)
            update_matrix = solve_spd(gram, new_gram)
            direction = residual + jnp.dot(
                update_matrix.T, direction, precision=lax.Precision.HIGHEST
            )
            gram = new_gram
    own_solution = lax.dynamic_slice_in_dim(solution, own_first, own_count, 1)
    own_residual = lax.dynamic_slice_in_dim(residual, own_first, own_count, 1)
    return (own_solution, own_residual)


def solution(mesh):
    placed = (
        P(None, ("task", "row", "col")),
        P(("task", "row", "col")),
        P(),
        P(),
        P(),
        P(),
        P(),
        P(None, ("task", "row", "col")),
        P("task", None),
        P("task"),
        P("task"),
    )
    return jax.shard_map(
        on_device,
        mesh=mesh,
        in_specs=placed,
        out_specs=(P(None, ("task", "row", "col")), P(None, ("task", "row", "col"))),
        check_vma=False,
    )
```

```python
import jax
import jax.numpy as jnp
from jax import lax
from jax.sharding import PartitionSpec as P

ITERS = 2


def fidelity_matrix(fidelity_factor):
    lower = jnp.tril(fidelity_factor)
    return jnp.dot(lower, lower.T, precision=lax.Precision.HIGHEST) + 0.5 * jnp.eye(
        fidelity_factor.shape[0], dtype=jnp.float32
    )


def left_product(weights, values):
    return lax.dot_general(
        weights, values, (((0,), (0,)), ((), ())), preferred_element_type=jnp.float32
    )


def outer_gram(left_side, right_side):
    return lax.dot_general(
        left_side, right_side, (((1,), (1,)), ((), ())), precision=lax.Precision.HIGHEST
    )


def solve_spd(matrix, right_side):
    return jax.scipy.linalg.cho_solve((jnp.linalg.cholesky(matrix), True), right_side)


def block_size(total_count, largest):
    chosen = min(total_count, largest)
    while total_count % chosen != 0:
        chosen = chosen - 1
    return chosen


def rung_fidelity(fidelity, rung_value):
    levels = jnp.arange(fidelity.shape[0], dtype=jnp.float32)
    onehot = (rung_value.astype(jnp.float32)[None, :] == levels[:, None]).astype(jnp.float32)
    return jnp.dot(fidelity, onehot, precision=lax.Precision.HIGHEST)


def split_three(values):
    first = lax.reduce_precision(values, exponent_bits=8, mantissa_bits=7)
    rest = values - first
    second = lax.reduce_precision(rest, exponent_bits=8, mantissa_bits=7)
    third = lax.reduce_precision(rest - second, exponent_bits=8, mantissa_bits=7)
    return (
        first.astype(jnp.bfloat16),
        second.astype(jnp.bfloat16),
        third.astype(jnp.bfloat16),
    )


def split_product(direction, kernel):
    count = direction.shape[0]
    d_one, d_two, d_three = split_three(direction)
    k_one, k_two, k_three = split_three(kernel)
    dims = (((1,), (1,)), ((), ()))
    by_first = lax.dot_general(
        jnp.concatenate([d_one, d_two, d_three], axis=0), k_one, dims,
        preferred_element_type=jnp.float32,
    )
    by_second = lax.dot_general(
        jnp.concatenate([d_one, d_two], axis=0), k_two, dims, preferred_element_type=jnp.float32
    )
    by_third = lax.dot_general(d_one, k_three, dims, preferred_element_type=jnp.float32)
    return (
        by_first[:count]
        + by_first[count : 2 * count]
        + by_first[2 * count :]
        + by_second[:count]
        + by_second[count:]
        + by_third
    )


def kernel_image(embedding, squares, rung_value, col_fidelity, inverse_scale, direction):
    count = embedding.shape[1]
    row_block = block_size(count, 2048)
    col_block = block_size(count, 2048)
    levels = jnp.arange(col_fidelity.shape[0], dtype=jnp.float32)

    def one_row_block(block_number):
        first_row = block_number * row_block
        rows_embedding = lax.dynamic_slice_in_dim(embedding, first_row, row_block, 1)
        rows_squares = lax.dynamic_slice_in_dim(squares, first_row, row_block, 0)
        rows_rung = lax.dynamic_slice_in_dim(rung_value, first_row, row_block, 0)
        rows_match = rows_rung.astype(jnp.float32)[:, None] == levels[None, :]

        def one_col_block(running, column_number):
            first_col = column_number * col_block
            cols_embedding = lax.dynamic_slice_in_dim(embedding, first_col, col_block, 1)
            cols_squares = lax.dynamic_slice_in_dim(squares, first_col, col_block, 0)
            cols_fidelity = lax.dynamic_slice_in_dim(col_fidelity, first_col, col_block, 1)
            cols_direction = lax.dynamic_slice_in_dim(direction, first_col, col_block, 1)
            inner = left_product(rows_embedding, cols_embedding)
            distance = rows_squares[:, None] + cols_squares[None, :] - 2.0 * inner
            tile_fidelity = cols_fidelity[0][None, :]
            for level in range(1, col_fidelity.shape[0]):
                tile_fidelity = jnp.where(
                    rows_match[:, level : level + 1], cols_fidelity[level][None, :], tile_fidelity
                )
            kernel = jnp.exp(-inverse_scale[0] * distance) * tile_fidelity
            contribution = split_product(cols_direction, kernel)
            return (running + contribution, None)

        start_value = jnp.zeros((direction.shape[0], row_block), jnp.float32)
        result, unused = lax.scan(
            one_col_block, start_value, jnp.arange(count // col_block, dtype=jnp.int32)
        )
        return result

    stacked = lax.map(one_row_block, jnp.arange(count // row_block, dtype=jnp.int32))
    return jnp.transpose(stacked, (1, 0, 2)).reshape(direction.shape[0], count)


def on_device(
    features,
    rung_index,
    w_first,
    b_first,
    w_second,
    b_second,
    w_third,
    targets,
    fidelity_factor,
    inverse_scale,
    noise_var,
):
    fidelity = fidelity_matrix(fidelity_factor)
    hidden_one = jax.nn.silu(left_product(w_first, features) + b_first[:, None]).astype(
        jnp.bfloat16
    )
    hidden_two = jax.nn.silu(left_product(w_second, hidden_one) + b_second[:, None]).astype(
        jnp.bfloat16
    )
    embedding = left_product(w_third, hidden_two).astype(jnp.bfloat16)
    rung_value = rung_index.astype(jnp.float32).astype(jnp.bfloat16)
    own_count = targets.shape[1]
    own_first = (lax.axis_index("row") * lax.axis_size("col") + lax.axis_index("col")) * own_count

    emb_rows = embedding.shape[0]
    packed = jnp.concatenate(
        [embedding.astype(jnp.float32), targets, rung_value.astype(jnp.float32)[None, :]], axis=0
    )
    gathered = lax.all_gather(packed, ("row", "col"), axis=1, tiled=True)
    all_embedding = gathered[:emb_rows].astype(jnp.bfloat16)
    all_targets = gathered[emb_rows : emb_rows + targets.shape[0]]
    all_rung = gathered[emb_rows + targets.shape[0]]

    squares = jnp.sum(jnp.square(all_embedding.astype(jnp.float32)), axis=0)
    col_fidelity = rung_fidelity(fidelity, all_rung)

    solution = jnp.zeros_like(all_targets)
    residual = all_targets
    direction = all_targets
    gram = outer_gram(residual, residual)
    for iteration in range(ITERS):
        image = (
            kernel_image(all_embedding, squares, all_rung, col_fidelity, inverse_scale, direction)
            + noise_var[0] * direction
        )
        curvature = outer_gram(direction, image)
        step_matrix = solve_spd(curvature, gram)
        solution = solution + jnp.dot(step_matrix.T, direction, precision=lax.Precision.HIGHEST)
        residual = residual - jnp.dot(step_matrix.T, image, precision=lax.Precision.HIGHEST)
        if iteration + 1 < ITERS:
            new_gram = outer_gram(residual, residual)
            update_matrix = solve_spd(gram, new_gram)
            direction = residual + jnp.dot(
                update_matrix.T, direction, precision=lax.Precision.HIGHEST
            )
            gram = new_gram
    own_solution = lax.dynamic_slice_in_dim(solution, own_first, own_count, 1)
    own_residual = lax.dynamic_slice_in_dim(residual, own_first, own_count, 1)
    return (own_solution, own_residual)


def solution(mesh):
    placed = (
        P(None, ("task", "row", "col")),
        P(("task", "row", "col")),
        P(),
        P(),
        P(),
        P(),
        P(),
        P(None, ("task", "row", "col")),
        P("task", None),
        P("task"),
        P("task"),
    )
    return jax.shard_map(
        on_device,
        mesh=mesh,
        in_specs=placed,
        out_specs=(P(None, ("task", "row", "col")), P(None, ("task", "row", "col"))),
        check_vma=False,
    )
```

```python
import jax
import jax.numpy as jnp
from jax import lax
from jax.sharding import PartitionSpec as P

ITERS = 2


def fidelity_matrix(fidelity_factor):
    lower = jnp.tril(fidelity_factor)
    return jnp.dot(lower, lower.T, precision=lax.Precision.HIGHEST) + 0.5 * jnp.eye(
        fidelity_factor.shape[0], dtype=jnp.float32
    )


def left_product(weights, values):
    return lax.dot_general(
        weights, values, (((0,), (0,)), ((), ())), preferred_element_type=jnp.float32
    )


def outer_gram(left_side, right_side):
    return lax.dot_general(
        left_side, right_side, (((1,), (1,)), ((), ())), precision=lax.Precision.HIGHEST
    )


def solve_spd(matrix, right_side):
    return jax.scipy.linalg.cho_solve((jnp.linalg.cholesky(matrix), True), right_side)


def block_size(total_count, largest):
    chosen = min(total_count, largest)
    while total_count % chosen != 0:
        chosen = chosen - 1
    return chosen


def rung_fidelity(fidelity, rung_value):
    levels = jnp.arange(fidelity.shape[0], dtype=jnp.float32)
    onehot = (rung_value.astype(jnp.float32)[None, :] == levels[:, None]).astype(jnp.float32)
    return jnp.dot(fidelity, onehot, precision=lax.Precision.HIGHEST)


def split_three(values):
    first = lax.reduce_precision(values, exponent_bits=8, mantissa_bits=7)
    rest = values - first
    second = lax.reduce_precision(rest, exponent_bits=8, mantissa_bits=7)
    third = lax.reduce_precision(rest - second, exponent_bits=8, mantissa_bits=7)
    return (
        first.astype(jnp.bfloat16),
        second.astype(jnp.bfloat16),
        third.astype(jnp.bfloat16),
    )


def split_product(direction, kernel):
    count = direction.shape[0]
    d_one, d_two, d_three = split_three(direction)
    k_one, k_two, k_three = split_three(kernel)
    dims = (((1,), (1,)), ((), ()))
    by_first = lax.dot_general(
        jnp.concatenate([d_one, d_two, d_three], axis=0), k_one, dims,
        preferred_element_type=jnp.float32,
    )
    by_second = lax.dot_general(
        jnp.concatenate([d_one, d_two], axis=0), k_two, dims, preferred_element_type=jnp.float32
    )
    by_third = lax.dot_general(d_one, k_three, dims, preferred_element_type=jnp.float32)
    return (
        by_first[:count]
        + by_first[count : 2 * count]
        + by_first[2 * count :]
        + by_second[:count]
        + by_second[count:]
        + by_third
    )


def kernel_image(embedding, squares, rung_value, col_fidelity, inverse_scale, direction):
    count = embedding.shape[1]
    row_block = block_size(count, 2048)
    col_block = block_size(count, 2048)
    levels = jnp.arange(col_fidelity.shape[0], dtype=jnp.float32)

    def one_row_block(block_number):
        first_row = block_number * row_block
        rows_embedding = lax.dynamic_slice_in_dim(embedding, first_row, row_block, 1)
        rows_squares = lax.dynamic_slice_in_dim(squares, first_row, row_block, 0)
        rows_rung = lax.dynamic_slice_in_dim(rung_value, first_row, row_block, 0)
        rows_match = rows_rung.astype(jnp.float32)[:, None] == levels[None, :]

        def one_col_block(running, column_number):
            first_col = column_number * col_block
            cols_embedding = lax.dynamic_slice_in_dim(embedding, first_col, col_block, 1)
            cols_squares = lax.dynamic_slice_in_dim(squares, first_col, col_block, 0)
            cols_fidelity = lax.dynamic_slice_in_dim(col_fidelity, first_col, col_block, 1)
            cols_direction = lax.dynamic_slice_in_dim(direction, first_col, col_block, 1)
            inner = left_product(rows_embedding, cols_embedding)
            distance = rows_squares[:, None] + cols_squares[None, :] - 2.0 * inner
            tile_fidelity = cols_fidelity[0][None, :]
            for level in range(1, col_fidelity.shape[0]):
                tile_fidelity = jnp.where(
                    rows_match[:, level : level + 1], cols_fidelity[level][None, :], tile_fidelity
                )
            kernel = jnp.exp(-inverse_scale[0] * distance) * tile_fidelity
            contribution = lax.dot_general(
                cols_direction, kernel, (((1,), (1,)), ((), ())), precision=lax.Precision.HIGHEST
            )
            return (running + contribution, None)

        start_value = jnp.zeros((direction.shape[0], row_block), jnp.float32)
        result, unused = lax.scan(
            one_col_block, start_value, jnp.arange(count // col_block, dtype=jnp.int32)
        )
        return result

    stacked = lax.map(one_row_block, jnp.arange(count // row_block, dtype=jnp.int32))
    return jnp.transpose(stacked, (1, 0, 2)).reshape(direction.shape[0], count)


def on_device(
    features,
    rung_index,
    w_first,
    b_first,
    w_second,
    b_second,
    w_third,
    targets,
    fidelity_factor,
    inverse_scale,
    noise_var,
):
    fidelity = fidelity_matrix(fidelity_factor)
    hidden_one = jax.nn.silu(left_product(w_first, features) + b_first[:, None]).astype(
        jnp.bfloat16
    )
    hidden_two = jax.nn.silu(left_product(w_second, hidden_one) + b_second[:, None]).astype(
        jnp.bfloat16
    )
    embedding = left_product(w_third, hidden_two).astype(jnp.bfloat16)
    rung_value = rung_index.astype(jnp.float32).astype(jnp.bfloat16)
    own_count = targets.shape[1]
    own_first = (lax.axis_index("row") * lax.axis_size("col") + lax.axis_index("col")) * own_count

    emb_rows = embedding.shape[0]
    packed = jnp.concatenate(
        [embedding.astype(jnp.float32), targets, rung_value.astype(jnp.float32)[None, :]], axis=0
    )
    gathered = lax.all_gather(packed, ("row", "col"), axis=1, tiled=True)
    all_embedding = gathered[:emb_rows].astype(jnp.bfloat16)
    all_targets = gathered[emb_rows : emb_rows + targets.shape[0]]
    all_rung = gathered[emb_rows + targets.shape[0]]

    squares = jnp.sum(jnp.square(all_embedding.astype(jnp.float32)), axis=0)
    col_fidelity = rung_fidelity(fidelity, all_rung)

    solution = jnp.zeros_like(all_targets)
    residual = all_targets
    direction = all_targets
    gram = outer_gram(residual, residual)
    for iteration in range(ITERS):
        image = (
            kernel_image(all_embedding, squares, all_rung, col_fidelity, inverse_scale, direction)
            + noise_var[0] * direction
        )
        curvature = outer_gram(direction, image)
        step_matrix = solve_spd(curvature, gram)
        solution = solution + jnp.dot(step_matrix.T, direction, precision=lax.Precision.HIGHEST)
        residual = residual - jnp.dot(step_matrix.T, image, precision=lax.Precision.HIGHEST)
        if iteration + 1 < ITERS:
            new_gram = outer_gram(residual, residual)
            update_matrix = solve_spd(gram, new_gram)
            direction = residual + jnp.dot(
                update_matrix.T, direction, precision=lax.Precision.HIGHEST
            )
            gram = new_gram
    own_solution = lax.dynamic_slice_in_dim(solution, own_first, own_count, 1)
    own_residual = lax.dynamic_slice_in_dim(residual, own_first, own_count, 1)
    return (own_solution, own_residual)


def solution(mesh):
    placed = (
        P(None, ("task", "row", "col")),
        P(("task", "row", "col")),
        P(),
        P(),
        P(),
        P(),
        P(),
        P(None, ("task", "row", "col")),
        P("task", None),
        P("task"),
        P("task"),
    )
    return jax.shard_map(
        on_device,
        mesh=mesh,
        in_specs=placed,
        out_specs=(P(None, ("task", "row", "col")), P(None, ("task", "row", "col"))),
        check_vma=False,
    )
```

```python
import jax
import jax.numpy as jnp
from jax import lax
from jax.sharding import PartitionSpec as P

ITERS = 2


def fidelity_matrix(fidelity_factor):
    lower = jnp.tril(fidelity_factor)
    return jnp.dot(lower, lower.T, precision=lax.Precision.HIGHEST) + 0.5 * jnp.eye(
        fidelity_factor.shape[0], dtype=jnp.float32
    )


def left_product(weights, values):
    return lax.dot_general(
        weights, values, (((0,), (0,)), ((), ())), preferred_element_type=jnp.float32
    )


def outer_gram(left_side, right_side):
    return lax.dot_general(
        left_side, right_side, (((1,), (1,)), ((), ())), precision=lax.Precision.HIGHEST
    )


def solve_spd(matrix, right_side):
    return jax.scipy.linalg.cho_solve((jnp.linalg.cholesky(matrix), True), right_side)


def block_size(total_count, largest):
    chosen = min(total_count, largest)
    while total_count % chosen != 0:
        chosen = chosen - 1
    return chosen


def rung_fidelity(fidelity, rung_value):
    levels = jnp.arange(fidelity.shape[0], dtype=jnp.float32)
    onehot = (rung_value.astype(jnp.float32)[None, :] == levels[:, None]).astype(jnp.float32)
    return jnp.dot(fidelity, onehot, precision=lax.Precision.HIGHEST)


def kernel_image(embedding, squares, rung_value, col_fidelity, inverse_scale, direction):
    count = embedding.shape[1]
    row_block = block_size(count, 2048)
    col_block = block_size(count, 2048)
    levels = jnp.arange(col_fidelity.shape[0], dtype=jnp.float32)

    def one_row_block(block_number):
        first_row = block_number * row_block
        rows_embedding = lax.dynamic_slice_in_dim(embedding, first_row, row_block, 1)
        rows_squares = lax.dynamic_slice_in_dim(squares, first_row, row_block, 0)
        rows_rung = lax.dynamic_slice_in_dim(rung_value, first_row, row_block, 0)
        rows_match = rows_rung.astype(jnp.float32)[:, None] == levels[None, :]

        def one_col_block(running, column_number):
            first_col = column_number * col_block
            cols_embedding = lax.dynamic_slice_in_dim(embedding, first_col, col_block, 1)
            cols_squares = lax.dynamic_slice_in_dim(squares, first_col, col_block, 0)
            cols_fidelity = lax.dynamic_slice_in_dim(col_fidelity, first_col, col_block, 1)
            cols_direction = lax.dynamic_slice_in_dim(direction, first_col, col_block, 1)
            inner = left_product(rows_embedding, cols_embedding)
            distance = rows_squares[:, None] + cols_squares[None, :] - 2.0 * inner
            tile_fidelity = cols_fidelity[0][None, :]
            for level in range(1, col_fidelity.shape[0]):
                tile_fidelity = jnp.where(
                    rows_match[:, level : level + 1], cols_fidelity[level][None, :], tile_fidelity
                )
            kernel = jnp.exp(-inverse_scale[0] * distance) * tile_fidelity
            contribution = lax.dot_general(
                cols_direction, kernel, (((1,), (1,)), ((), ())), precision=lax.Precision.HIGH
            )
            return (running + contribution, None)

        start_value = jnp.zeros((direction.shape[0], row_block), jnp.float32)
        result, unused = lax.scan(
            one_col_block, start_value, jnp.arange(count // col_block, dtype=jnp.int32)
        )
        return result

    stacked = lax.map(one_row_block, jnp.arange(count // row_block, dtype=jnp.int32))
    return jnp.transpose(stacked, (1, 0, 2)).reshape(direction.shape[0], count)


def on_device(
    features,
    rung_index,
    w_first,
    b_first,
    w_second,
    b_second,
    w_third,
    targets,
    fidelity_factor,
    inverse_scale,
    noise_var,
):
    fidelity = fidelity_matrix(fidelity_factor)
    hidden_one = jax.nn.silu(left_product(w_first, features) + b_first[:, None]).astype(
        jnp.bfloat16
    )
    hidden_two = jax.nn.silu(left_product(w_second, hidden_one) + b_second[:, None]).astype(
        jnp.bfloat16
    )
    embedding = lax.reduce_precision(
        left_product(w_third, hidden_two), exponent_bits=8, mantissa_bits=7
    )
    rung_value = rung_index.astype(jnp.float32)
    own_count = targets.shape[1]
    own_first = (lax.axis_index("row") * lax.axis_size("col") + lax.axis_index("col")) * own_count

    emb_rows = embedding.shape[0]
    packed = jnp.concatenate(
        [embedding, targets, rung_value[None, :]], axis=0
    )
    gathered = lax.all_gather(packed, ("row", "col"), axis=1, tiled=True)
    all_embedding = gathered[:emb_rows].astype(jnp.bfloat16)
    all_targets = gathered[emb_rows : emb_rows + targets.shape[0]]
    all_rung = gathered[emb_rows + targets.shape[0]]

    squares = jnp.sum(jnp.square(gathered[:emb_rows]), axis=0)
    col_fidelity = rung_fidelity(fidelity, all_rung)

    solution = jnp.zeros_like(all_targets)
    residual = all_targets
    direction = all_targets
    gram = outer_gram(residual, residual)
    for iteration in range(ITERS):
        image = (
            kernel_image(all_embedding, squares, all_rung, col_fidelity, inverse_scale, direction)
            + noise_var[0] * direction
        )
        curvature = outer_gram(direction, image)
        step_matrix = solve_spd(curvature, gram)
        solution = solution + jnp.dot(step_matrix.T, direction, precision=lax.Precision.HIGHEST)
        residual = residual - jnp.dot(step_matrix.T, image, precision=lax.Precision.HIGHEST)
        if iteration + 1 < ITERS:
            new_gram = outer_gram(residual, residual)
            update_matrix = solve_spd(gram, new_gram)
            direction = residual + jnp.dot(
                update_matrix.T, direction, precision=lax.Precision.HIGHEST
            )
            gram = new_gram
    own_solution = lax.dynamic_slice_in_dim(solution, own_first, own_count, 1)
    own_residual = lax.dynamic_slice_in_dim(residual, own_first, own_count, 1)
    return (own_solution, own_residual)


def solution(mesh):
    placed = (
        P(None, ("task", "row", "col")),
        P(("task", "row", "col")),
        P(),
        P(),
        P(),
        P(),
        P(),
        P(None, ("task", "row", "col")),
        P("task", None),
        P("task"),
        P("task"),
    )
    return jax.shard_map(
        on_device,
        mesh=mesh,
        in_specs=placed,
        out_specs=(P(None, ("task", "row", "col")), P(None, ("task", "row", "col"))),
        check_vma=False,
    )
```

```python
import jax
import jax.numpy as jnp
from jax import lax
from jax.sharding import PartitionSpec as P
from jax.experimental import pallas as pl
from jax.experimental.pallas import tpu as pltpu

ITERS = 2


def fidelity_matrix(fidelity_factor):
    lower = jnp.tril(fidelity_factor)
    return jnp.dot(lower, lower.T, precision=lax.Precision.HIGHEST) + 0.5 * jnp.eye(
        fidelity_factor.shape[0], dtype=jnp.float32
    )


def left_product(weights, values):
    return lax.dot_general(
        weights, values, (((0,), (0,)), ((), ())), preferred_element_type=jnp.float32
    )


def outer_gram(left_side, right_side):
    return lax.dot_general(
        left_side, right_side, (((1,), (1,)), ((), ())), precision=lax.Precision.HIGHEST
    )


def solve_spd(matrix, right_side):
    return jax.scipy.linalg.cho_solve((jnp.linalg.cholesky(matrix), True), right_side)


def block_size(total_count, largest):
    chosen = min(total_count, largest)
    while total_count % chosen != 0:
        chosen = chosen - 1
    return chosen


def rung_fidelity(fidelity, rung_value):
    levels = jnp.arange(fidelity.shape[0], dtype=jnp.float32)
    onehot = (rung_value.astype(jnp.float32)[None, :] == levels[:, None]).astype(jnp.float32)
    return jnp.dot(fidelity, onehot, precision=lax.Precision.HIGHEST)


def image_block(rows_ref, cols_ref, cols_sq_ref, cols_fid_ref, dir_ref, scale_ref, out_ref):
    emb_rows = cols_ref.shape[0]
    rows_emb = rows_ref[:, :emb_rows].astype(jnp.bfloat16)
    rows_sq = rows_ref[:, emb_rows : emb_rows + 1]
    rows_rung = rows_ref[:, emb_rows + 1 : emb_rows + 2]
    inner = jnp.dot(rows_emb, cols_ref[...], preferred_element_type=jnp.float32)
    distance = rows_sq + cols_sq_ref[...] - 2.0 * inner
    cols_fid = cols_fid_ref[...]
    tile_fid = cols_fid[0:1, :]
    for level in range(1, cols_fid.shape[0]):
        tile_fid = jnp.where(rows_rung == float(level), cols_fid[level : level + 1, :], tile_fid)
    kernel = jnp.exp(scale_ref[...] * distance) * tile_fid
    kernel_hi = kernel.astype(jnp.bfloat16)
    kernel_lo = (kernel - kernel_hi.astype(jnp.float32)).astype(jnp.bfloat16)
    dims = (((1,), (1,)), ((), ()))
    both = dir_ref[...]
    count = out_ref.shape[0]
    by_hi = lax.dot_general(both, kernel_hi, dims, preferred_element_type=jnp.float32)
    by_lo = lax.dot_general(both[:count], kernel_lo, dims, preferred_element_type=jnp.float32)
    contribution = (by_hi[:count] + by_hi[count:]) + by_lo

    @pl.when(pl.program_id(1) == 0)
    def _():
        out_ref[...] = contribution

    @pl.when(pl.program_id(1) != 0)
    def _():
        out_ref[...] = out_ref[...] + contribution


def kernel_image(embedding, squares, rung_value, col_fidelity, inverse_scale, direction):
    emb_rows, count = embedding.shape
    rhs = direction.shape[0]
    row_block = block_size(count, 256)
    col_block = block_size(count, 2048)
    direction_hi = lax.reduce_precision(direction, exponent_bits=8, mantissa_bits=7)
    direction_lo = (direction - direction_hi).astype(jnp.bfloat16)
    stacked = jnp.concatenate([direction_hi.astype(jnp.bfloat16), direction_lo], axis=0)
    scale = jnp.reshape(-inverse_scale[0], (1, 1))
    grid = (count // row_block, count // col_block)
    row_width = 128 * ((emb_rows + 2 + 127) // 128)
    rows_packed = jnp.concatenate(
        [
            embedding,
            squares[None, :],
            rung_value[None, :],
            jnp.zeros((row_width - emb_rows - 2, count), jnp.float32),
        ],
        axis=0,
    ).T
    return pl.pallas_call(
        image_block,
        grid=grid,
        in_specs=[
            pl.BlockSpec((row_block, row_width), lambda i, j: (i, 0)),
            pl.BlockSpec((emb_rows, col_block), lambda i, j: (0, j)),
            pl.BlockSpec((1, col_block), lambda i, j: (0, j)),
            pl.BlockSpec((col_fidelity.shape[0], col_block), lambda i, j: (0, j)),
            pl.BlockSpec((2 * rhs, col_block), lambda i, j: (0, j)),
            pl.BlockSpec((1, 1), lambda i, j: (0, 0)),
        ],
        out_specs=pl.BlockSpec((rhs, row_block), lambda i, j: (0, i)),
        out_shape=jax.ShapeDtypeStruct((rhs, count), jnp.float32),
    )(
        rows_packed,
        embedding.astype(jnp.bfloat16),
        squares[None, :],
        col_fidelity,
        stacked,
        scale,
    )


def on_device(
    features,
    rung_index,
    w_first,
    b_first,
    w_second,
    b_second,
    w_third,
    targets,
    fidelity_factor,
    inverse_scale,
    noise_var,
):
    fidelity = fidelity_matrix(fidelity_factor)
    hidden_one = jax.nn.silu(left_product(w_first, features) + b_first[:, None]).astype(
        jnp.bfloat16
    )
    hidden_two = jax.nn.silu(left_product(w_second, hidden_one) + b_second[:, None]).astype(
        jnp.bfloat16
    )
    embedding = lax.reduce_precision(
        left_product(w_third, hidden_two), exponent_bits=8, mantissa_bits=7
    )
    rung_value = rung_index.astype(jnp.float32)
    own_count = targets.shape[1]
    own_first = (lax.axis_index("row") * lax.axis_size("col") + lax.axis_index("col")) * own_count

    emb_rows = embedding.shape[0]
    packed = jnp.concatenate(
        [embedding, targets, rung_value[None, :]], axis=0
    )
    gathered = lax.all_gather(packed, ("row", "col"), axis=1, tiled=True)
    all_embedding = gathered[:emb_rows].astype(jnp.bfloat16)
    all_targets = gathered[emb_rows : emb_rows + targets.shape[0]]
    all_rung = gathered[emb_rows + targets.shape[0]]

    squares = jnp.sum(jnp.square(gathered[:emb_rows]), axis=0)
    col_fidelity = rung_fidelity(fidelity, all_rung)

    solution = jnp.zeros_like(all_targets)
    residual = all_targets
    direction = all_targets
    gram = outer_gram(residual, residual)
    for iteration in range(ITERS):
        image = (
            kernel_image(
                gathered[:emb_rows], squares, all_rung, col_fidelity, inverse_scale, direction
            )
            + noise_var[0] * direction
        )
        curvature = outer_gram(direction, image)
        step_matrix = solve_spd(curvature, gram)
        solution = solution + jnp.dot(step_matrix.T, direction, precision=lax.Precision.HIGHEST)
        residual = residual - jnp.dot(step_matrix.T, image, precision=lax.Precision.HIGHEST)
        if iteration + 1 < ITERS:
            new_gram = outer_gram(residual, residual)
            update_matrix = solve_spd(gram, new_gram)
            direction = residual + jnp.dot(
                update_matrix.T, direction, precision=lax.Precision.HIGHEST
            )
            gram = new_gram
    own_solution = lax.dynamic_slice_in_dim(solution, own_first, own_count, 1)
    own_residual = lax.dynamic_slice_in_dim(residual, own_first, own_count, 1)
    return (own_solution, own_residual)


def solution(mesh):
    placed = (
        P(None, ("task", "row", "col")),
        P(("task", "row", "col")),
        P(),
        P(),
        P(),
        P(),
        P(),
        P(None, ("task", "row", "col")),
        P("task", None),
        P("task"),
        P("task"),
    )
    return jax.shard_map(
        on_device,
        mesh=mesh,
        in_specs=placed,
        out_specs=(P(None, ("task", "row", "col")), P(None, ("task", "row", "col"))),
        check_vma=False,
    )
```

```python
import jax
import jax.numpy as jnp
from jax import lax
from jax.sharding import PartitionSpec as P
from jax.experimental import pallas as pl
from jax.experimental.pallas import tpu as pltpu

ITERS = 2


def fidelity_matrix(fidelity_factor):
    lower = jnp.tril(fidelity_factor)
    return jnp.dot(lower, lower.T, precision=lax.Precision.HIGHEST) + 0.5 * jnp.eye(
        fidelity_factor.shape[0], dtype=jnp.float32
    )


def left_product(weights, values):
    return lax.dot_general(
        weights, values, (((0,), (0,)), ((), ())), preferred_element_type=jnp.float32
    )


def outer_gram(left_side, right_side):
    return lax.dot_general(
        left_side, right_side, (((1,), (1,)), ((), ())), precision=lax.Precision.HIGHEST
    )


def solve_spd(matrix, right_side):
    return jax.scipy.linalg.cho_solve((jnp.linalg.cholesky(matrix), True), right_side)


def block_size(total_count, largest):
    chosen = min(total_count, largest)
    while total_count % chosen != 0:
        chosen = chosen - 1
    return chosen


def rung_fidelity(fidelity, rung_value):
    levels = jnp.arange(fidelity.shape[0], dtype=jnp.float32)
    onehot = (rung_value.astype(jnp.float32)[None, :] == levels[:, None]).astype(jnp.float32)
    return jnp.dot(fidelity, onehot, precision=lax.Precision.HIGHEST)


def image_block(sum_ref, out_emb_ref, out_sq_ref, out_fid_ref, dir_ref, scale_ref, out_ref):
    emb_rows = out_emb_ref.shape[0]
    sum_emb = sum_ref[:, :emb_rows].astype(jnp.bfloat16)
    sum_sq = sum_ref[:, emb_rows : emb_rows + 1]
    sum_rung = sum_ref[:, emb_rows + 1 : emb_rows + 2]
    inner = jnp.dot(sum_emb, out_emb_ref[...], preferred_element_type=jnp.float32)
    distance = out_sq_ref[...] + sum_sq - 2.0 * inner
    out_fid = out_fid_ref[...]
    tile_fid = out_fid[0:1, :]
    for level in range(1, out_fid.shape[0]):
        tile_fid = jnp.where(sum_rung == float(level), out_fid[level : level + 1, :], tile_fid)
    kernel = jnp.exp(scale_ref[...] * distance) * tile_fid
    kernel_hi = kernel.astype(jnp.bfloat16)
    kernel_lo = (kernel - kernel_hi.astype(jnp.float32)).astype(jnp.bfloat16)
    both = dir_ref[...]
    count = out_ref.shape[0]
    by_hi = jnp.dot(both, kernel_hi, preferred_element_type=jnp.float32)
    by_lo = jnp.dot(both[:count], kernel_lo, preferred_element_type=jnp.float32)
    contribution = (by_hi[:count] + by_hi[count:]) + by_lo

    @pl.when(pl.program_id(1) == 0)
    def _():
        out_ref[...] = contribution

    @pl.when(pl.program_id(1) != 0)
    def _():
        out_ref[...] = out_ref[...] + contribution


def kernel_image(embedding, squares, rung_value, col_fidelity, inverse_scale, direction):
    emb_rows, count = embedding.shape
    rhs = direction.shape[0]
    out_block = block_size(count, 256)
    sum_block = block_size(count, 2048)
    direction_hi = lax.reduce_precision(direction, exponent_bits=8, mantissa_bits=7)
    direction_lo = (direction - direction_hi).astype(jnp.bfloat16)
    stacked = jnp.concatenate([direction_hi.astype(jnp.bfloat16), direction_lo], axis=0)
    scale = jnp.reshape(-inverse_scale[0], (1, 1))
    grid = (count // out_block, count // sum_block)
    sum_width = 128 * ((emb_rows + 2 + 127) // 128)
    sum_packed = jnp.concatenate(
        [
            embedding,
            squares[None, :],
            rung_value[None, :],
            jnp.zeros((sum_width - emb_rows - 2, count), jnp.float32),
        ],
        axis=0,
    ).T
    return pl.pallas_call(
        image_block,
        grid=grid,
        in_specs=[
            pl.BlockSpec((sum_block, sum_width), lambda i, j: (j, 0)),
            pl.BlockSpec((emb_rows, out_block), lambda i, j: (0, i)),
            pl.BlockSpec((1, out_block), lambda i, j: (0, i)),
            pl.BlockSpec((col_fidelity.shape[0], out_block), lambda i, j: (0, i)),
            pl.BlockSpec((2 * rhs, sum_block), lambda i, j: (0, j)),
            pl.BlockSpec((1, 1), lambda i, j: (0, 0)),
        ],
        out_specs=pl.BlockSpec((rhs, out_block), lambda i, j: (0, i)),
        out_shape=jax.ShapeDtypeStruct((rhs, count), jnp.float32),
    )(
        sum_packed,
        embedding.astype(jnp.bfloat16),
        squares[None, :],
        col_fidelity,
        stacked,
        scale,
    )


def on_device(
    features,
    rung_index,
    w_first,
    b_first,
    w_second,
    b_second,
    w_third,
    targets,
    fidelity_factor,
    inverse_scale,
    noise_var,
):
    fidelity = fidelity_matrix(fidelity_factor)
    hidden_one = jax.nn.silu(left_product(w_first, features) + b_first[:, None]).astype(
        jnp.bfloat16
    )
    hidden_two = jax.nn.silu(left_product(w_second, hidden_one) + b_second[:, None]).astype(
        jnp.bfloat16
    )
    embedding = lax.reduce_precision(
        left_product(w_third, hidden_two), exponent_bits=8, mantissa_bits=7
    )
    rung_value = rung_index.astype(jnp.float32)
    own_count = targets.shape[1]
    own_first = (lax.axis_index("row") * lax.axis_size("col") + lax.axis_index("col")) * own_count

    emb_rows = embedding.shape[0]
    packed = jnp.concatenate(
        [embedding, targets, rung_value[None, :]], axis=0
    )
    gathered = lax.all_gather(packed, ("row", "col"), axis=1, tiled=True)
    all_embedding = gathered[:emb_rows].astype(jnp.bfloat16)
    all_targets = gathered[emb_rows : emb_rows + targets.shape[0]]
    all_rung = gathered[emb_rows + targets.shape[0]]

    squares = jnp.sum(jnp.square(gathered[:emb_rows]), axis=0)
    col_fidelity = rung_fidelity(fidelity, all_rung)

    solution = jnp.zeros_like(all_targets)
    residual = all_targets
    direction = all_targets
    gram = outer_gram(residual, residual)
    for iteration in range(ITERS):
        image = (
            kernel_image(
                gathered[:emb_rows], squares, all_rung, col_fidelity, inverse_scale, direction
            )
            + noise_var[0] * direction
        )
        curvature = outer_gram(direction, image)
        step_matrix = solve_spd(curvature, gram)
        solution = solution + jnp.dot(step_matrix.T, direction, precision=lax.Precision.HIGHEST)
        residual = residual - jnp.dot(step_matrix.T, image, precision=lax.Precision.HIGHEST)
        if iteration + 1 < ITERS:
            new_gram = outer_gram(residual, residual)
            update_matrix = solve_spd(gram, new_gram)
            direction = residual + jnp.dot(
                update_matrix.T, direction, precision=lax.Precision.HIGHEST
            )
            gram = new_gram
    own_solution = lax.dynamic_slice_in_dim(solution, own_first, own_count, 1)
    own_residual = lax.dynamic_slice_in_dim(residual, own_first, own_count, 1)
    return (own_solution, own_residual)


def solution(mesh):
    placed = (
        P(None, ("task", "row", "col")),
        P(("task", "row", "col")),
        P(),
        P(),
        P(),
        P(),
        P(),
        P(None, ("task", "row", "col")),
        P("task", None),
        P("task"),
        P("task"),
    )
    return jax.shard_map(
        on_device,
        mesh=mesh,
        in_specs=placed,
        out_specs=(P(None, ("task", "row", "col")), P(None, ("task", "row", "col"))),
        check_vma=False,
    )
```

```python
import jax
import jax.numpy as jnp
from jax import lax
from jax.sharding import PartitionSpec as P

ITERS = 2


def fidelity_matrix(fidelity_factor):
    lower = jnp.tril(fidelity_factor)
    return jnp.dot(lower, lower.T, precision=lax.Precision.HIGHEST) + 0.5 * jnp.eye(
        fidelity_factor.shape[0], dtype=jnp.float32
    )


def left_product(weights, values):
    return lax.dot_general(
        weights, values, (((0,), (0,)), ((), ())), preferred_element_type=jnp.float32
    )


def outer_gram(left_side, right_side):
    return lax.dot_general(
        left_side, right_side, (((1,), (1,)), ((), ())), precision=lax.Precision.HIGHEST
    )


def solve_spd(matrix, right_side):
    return jax.scipy.linalg.cho_solve((jnp.linalg.cholesky(matrix), True), right_side)


def block_size(total_count, largest):
    chosen = min(total_count, largest)
    while total_count % chosen != 0:
        chosen = chosen - 1
    return chosen


def rung_fidelity(fidelity, rung_value):
    levels = jnp.arange(fidelity.shape[0], dtype=jnp.float32)
    onehot = (rung_value.astype(jnp.float32)[None, :] == levels[:, None]).astype(jnp.float32)
    return jnp.dot(fidelity, onehot, precision=lax.Precision.HIGHEST)


def split_two(values):
    high = lax.reduce_precision(values, exponent_bits=8, mantissa_bits=7)
    return high.astype(jnp.bfloat16), (values - high).astype(jnp.bfloat16)


def split_product(direction, kernel):
    count = direction.shape[0]
    d_high, d_low = split_two(direction)
    k_high, k_low = split_two(kernel)
    dims = (((1,), (1,)), ((), ()))
    by_high = lax.dot_general(
        jnp.concatenate([d_high, d_low], axis=0), k_high, dims,
        preferred_element_type=jnp.float32,
    )
    by_low = lax.dot_general(d_high, k_low, dims, preferred_element_type=jnp.float32)
    return (by_high[:count] + by_high[count:]) + by_low


def kernel_image(embedding, squares, rung_value, col_fidelity, inverse_scale, direction):
    count = embedding.shape[1]
    row_block = block_size(count, 2048)
    col_block = block_size(count, 2048)
    levels = jnp.arange(col_fidelity.shape[0], dtype=jnp.float32)

    def one_row_block(block_number):
        first_row = block_number * row_block
        rows_embedding = lax.dynamic_slice_in_dim(embedding, first_row, row_block, 1)
        rows_squares = lax.dynamic_slice_in_dim(squares, first_row, row_block, 0)
        rows_rung = lax.dynamic_slice_in_dim(rung_value, first_row, row_block, 0)
        rows_match = rows_rung.astype(jnp.float32)[:, None] == levels[None, :]

        def one_col_block(running, column_number):
            first_col = column_number * col_block
            cols_embedding = lax.dynamic_slice_in_dim(embedding, first_col, col_block, 1)
            cols_squares = lax.dynamic_slice_in_dim(squares, first_col, col_block, 0)
            cols_fidelity = lax.dynamic_slice_in_dim(col_fidelity, first_col, col_block, 1)
            cols_direction = lax.dynamic_slice_in_dim(direction, first_col, col_block, 1)
            inner = left_product(rows_embedding, cols_embedding)
            distance = rows_squares[:, None] + cols_squares[None, :] - 2.0 * inner
            tile_fidelity = cols_fidelity[0][None, :]
            for level in range(1, col_fidelity.shape[0]):
                tile_fidelity = jnp.where(
                    rows_match[:, level : level + 1], cols_fidelity[level][None, :], tile_fidelity
                )
            kernel = jnp.exp(-inverse_scale[0] * distance) * tile_fidelity
            contribution = split_product(cols_direction, kernel)
            return (running + contribution, None)

        start_value = jnp.zeros((direction.shape[0], row_block), jnp.float32)
        result, unused = lax.scan(
            one_col_block, start_value, jnp.arange(count // col_block, dtype=jnp.int32)
        )
        return result

    stacked = lax.map(one_row_block, jnp.arange(count // row_block, dtype=jnp.int32))
    return jnp.transpose(stacked, (1, 0, 2)).reshape(direction.shape[0], count)


def on_device(
    features,
    rung_index,
    w_first,
    b_first,
    w_second,
    b_second,
    w_third,
    targets,
    fidelity_factor,
    inverse_scale,
    noise_var,
):
    fidelity = fidelity_matrix(fidelity_factor)
    hidden_one = jax.nn.silu(left_product(w_first, features) + b_first[:, None]).astype(
        jnp.bfloat16
    )
    hidden_two = jax.nn.silu(left_product(w_second, hidden_one) + b_second[:, None]).astype(
        jnp.bfloat16
    )
    embedding = lax.reduce_precision(
        left_product(w_third, hidden_two), exponent_bits=8, mantissa_bits=7
    )
    rung_value = rung_index.astype(jnp.float32)
    own_count = targets.shape[1]
    own_first = (lax.axis_index("row") * lax.axis_size("col") + lax.axis_index("col")) * own_count

    emb_rows = embedding.shape[0]
    packed = jnp.concatenate(
        [embedding, targets, rung_value[None, :]], axis=0
    )
    gathered = lax.all_gather(packed, ("row", "col"), axis=1, tiled=True)
    all_embedding = gathered[:emb_rows].astype(jnp.bfloat16)
    all_targets = gathered[emb_rows : emb_rows + targets.shape[0]]
    all_rung = gathered[emb_rows + targets.shape[0]]

    squares = jnp.sum(jnp.square(gathered[:emb_rows]), axis=0)
    col_fidelity = rung_fidelity(fidelity, all_rung)

    solution = jnp.zeros_like(all_targets)
    residual = all_targets
    direction = all_targets
    gram = outer_gram(residual, residual)
    for iteration in range(ITERS):
        image = (
            kernel_image(all_embedding, squares, all_rung, col_fidelity, inverse_scale, direction)
            + noise_var[0] * direction
        )
        curvature = outer_gram(direction, image)
        step_matrix = solve_spd(curvature, gram)
        solution = solution + jnp.dot(step_matrix.T, direction, precision=lax.Precision.HIGHEST)
        residual = residual - jnp.dot(step_matrix.T, image, precision=lax.Precision.HIGHEST)
        if iteration + 1 < ITERS:
            new_gram = outer_gram(residual, residual)
            update_matrix = solve_spd(gram, new_gram)
            direction = residual + jnp.dot(
                update_matrix.T, direction, precision=lax.Precision.HIGHEST
            )
            gram = new_gram
    own_solution = lax.dynamic_slice_in_dim(solution, own_first, own_count, 1)
    own_residual = lax.dynamic_slice_in_dim(residual, own_first, own_count, 1)
    return (own_solution, own_residual)


def solution(mesh):
    placed = (
        P(None, ("task", "row", "col")),
        P(("task", "row", "col")),
        P(),
        P(),
        P(),
        P(),
        P(),
        P(None, ("task", "row", "col")),
        P("task", None),
        P("task"),
        P("task"),
    )
    return jax.shard_map(
        on_device,
        mesh=mesh,
        in_specs=placed,
        out_specs=(P(None, ("task", "row", "col")), P(None, ("task", "row", "col"))),
        check_vma=False,
    )
```

```python
import jax
import jax.numpy as jnp
from jax import lax
from jax.sharding import PartitionSpec as P
from jax.experimental import pallas as pl

ITERS = 2


def fidelity_matrix(fidelity_factor):
    lower = jnp.tril(fidelity_factor)
    return jnp.dot(lower, lower.T, precision=lax.Precision.HIGHEST) + 0.5 * jnp.eye(
        fidelity_factor.shape[0], dtype=jnp.float32
    )


def left_product(weights, values):
    return lax.dot_general(
        weights, values, (((0,), (0,)), ((), ())), preferred_element_type=jnp.float32
    )


def outer_gram(left_side, right_side):
    return lax.dot_general(
        left_side, right_side, (((1,), (1,)), ((), ())), precision=lax.Precision.HIGHEST
    )


def cholesky_solve_block(matrix_ref, right_ref, out_ref):
    size = matrix_ref.shape[0]
    work = matrix_ref[...]
    rows = lax.broadcasted_iota(jnp.int32, (size, size), 0)
    cols = lax.broadcasted_iota(jnp.int32, (size, size), 1)
    row_index = rows[:, 0:1]
    col_index = cols[0:1, :]
    right_rows = lax.broadcasted_iota(jnp.int32, right_ref.shape, 0)
    lower = jnp.zeros((size, size), jnp.float32)
    upper = jnp.zeros((size, size), jnp.float32)
    for j in range(size):
        column = jnp.sum(jnp.where(cols == j, work, 0.0), axis=1, keepdims=True)
        row = jnp.sum(jnp.where(rows == j, work, 0.0), axis=0, keepdims=True)
        pivot = jnp.sum(jnp.where(col_index == j, row, 0.0), axis=1, keepdims=True)
        root = jnp.sqrt(pivot)
        column = jnp.where(row_index >= j, column / root, 0.0)
        row = jnp.where(col_index >= j, row / root, 0.0)
        lower = lower + jnp.where(cols == j, column, 0.0)
        upper = upper + jnp.where(rows == j, row, 0.0)
        work = work - column * row
    solved = right_ref[...]
    for j in range(size):
        column = jnp.sum(jnp.where(cols == j, lower, 0.0), axis=1, keepdims=True)
        diagonal = jnp.sum(jnp.where(row_index == j, column, 0.0), axis=0, keepdims=True)
        picked = jnp.sum(jnp.where(right_rows == j, solved, 0.0), axis=0, keepdims=True)
        value = picked / diagonal
        below = jnp.where(row_index > j, column, 0.0)
        solved = jnp.where(right_rows == j, value, solved - below * value)
    for j in reversed(range(size)):
        column = jnp.sum(jnp.where(cols == j, upper, 0.0), axis=1, keepdims=True)
        diagonal = jnp.sum(jnp.where(row_index == j, column, 0.0), axis=0, keepdims=True)
        picked = jnp.sum(jnp.where(right_rows == j, solved, 0.0), axis=0, keepdims=True)
        value = picked / diagonal
        above = jnp.where(row_index < j, column, 0.0)
        solved = jnp.where(right_rows == j, value, solved - above * value)
    out_ref[...] = solved


def solve_spd(matrix, right_side):
    symmetric = (matrix + matrix.T) / 2.0
    return pl.pallas_call(
        cholesky_solve_block,
        out_shape=jax.ShapeDtypeStruct(right_side.shape, jnp.float32),
    )(symmetric, right_side)


def block_size(total_count, largest):
    chosen = min(total_count, largest)
    while total_count % chosen != 0:
        chosen = chosen - 1
    return chosen


def rung_fidelity(fidelity, rung_value):
    levels = jnp.arange(fidelity.shape[0], dtype=jnp.float32)
    onehot = (rung_value.astype(jnp.float32)[None, :] == levels[:, None]).astype(jnp.float32)
    return jnp.dot(fidelity, onehot, precision=lax.Precision.HIGHEST)


def split_two(values):
    high = lax.reduce_precision(values, exponent_bits=8, mantissa_bits=7)
    return high.astype(jnp.bfloat16), (values - high).astype(jnp.bfloat16)


def split_product(direction, kernel):
    count = direction.shape[0]
    d_high, d_low = split_two(direction)
    k_high, k_low = split_two(kernel)
    dims = (((1,), (1,)), ((), ()))
    by_high = lax.dot_general(
        jnp.concatenate([d_high, d_low], axis=0), k_high, dims,
        preferred_element_type=jnp.float32,
    )
    by_low = lax.dot_general(d_high, k_low, dims, preferred_element_type=jnp.float32)
    return (by_high[:count] + by_high[count:]) + by_low


def kernel_image(embedding, squares, rung_value, col_fidelity, inverse_scale, direction):
    count = embedding.shape[1]
    row_block = block_size(count, 2048)
    col_block = block_size(count, 2048)
    levels = jnp.arange(col_fidelity.shape[0], dtype=jnp.float32)

    def one_row_block(block_number):
        first_row = block_number * row_block
        rows_embedding = lax.dynamic_slice_in_dim(embedding, first_row, row_block, 1)
        rows_squares = lax.dynamic_slice_in_dim(squares, first_row, row_block, 0)
        rows_rung = lax.dynamic_slice_in_dim(rung_value, first_row, row_block, 0)
        rows_match = rows_rung.astype(jnp.float32)[:, None] == levels[None, :]

        def one_col_block(running, column_number):
            first_col = column_number * col_block
            cols_embedding = lax.dynamic_slice_in_dim(embedding, first_col, col_block, 1)
            cols_squares = lax.dynamic_slice_in_dim(squares, first_col, col_block, 0)
            cols_fidelity = lax.dynamic_slice_in_dim(col_fidelity, first_col, col_block, 1)
            cols_direction = lax.dynamic_slice_in_dim(direction, first_col, col_block, 1)
            inner = left_product(rows_embedding, cols_embedding)
            distance = rows_squares[:, None] + cols_squares[None, :] - 2.0 * inner
            tile_fidelity = cols_fidelity[0][None, :]
            for level in range(1, col_fidelity.shape[0]):
                tile_fidelity = jnp.where(
                    rows_match[:, level : level + 1], cols_fidelity[level][None, :], tile_fidelity
                )
            kernel = jnp.exp(-inverse_scale[0] * distance) * tile_fidelity
            contribution = split_product(cols_direction, kernel)
            return (running + contribution, None)

        start_value = jnp.zeros((direction.shape[0], row_block), jnp.float32)
        result, unused = lax.scan(
            one_col_block, start_value, jnp.arange(count // col_block, dtype=jnp.int32)
        )
        return result

    stacked = lax.map(one_row_block, jnp.arange(count // row_block, dtype=jnp.int32))
    return jnp.transpose(stacked, (1, 0, 2)).reshape(direction.shape[0], count)


def on_device(
    features,
    rung_index,
    w_first,
    b_first,
    w_second,
    b_second,
    w_third,
    targets,
    fidelity_factor,
    inverse_scale,
    noise_var,
):
    fidelity = fidelity_matrix(fidelity_factor)
    hidden_one = jax.nn.silu(left_product(w_first, features) + b_first[:, None]).astype(
        jnp.bfloat16
    )
    hidden_two = jax.nn.silu(left_product(w_second, hidden_one) + b_second[:, None]).astype(
        jnp.bfloat16
    )
    embedding = lax.reduce_precision(
        left_product(w_third, hidden_two), exponent_bits=8, mantissa_bits=7
    )
    rung_value = rung_index.astype(jnp.float32)
    own_count = targets.shape[1]
    own_first = (lax.axis_index("row") * lax.axis_size("col") + lax.axis_index("col")) * own_count

    emb_rows = embedding.shape[0]
    packed = jnp.concatenate(
        [embedding, targets, rung_value[None, :]], axis=0
    )
    gathered = lax.all_gather(packed, ("row", "col"), axis=1, tiled=True)
    all_embedding = gathered[:emb_rows].astype(jnp.bfloat16)
    all_targets = gathered[emb_rows : emb_rows + targets.shape[0]]
    all_rung = gathered[emb_rows + targets.shape[0]]

    squares = jnp.sum(jnp.square(gathered[:emb_rows]), axis=0)
    col_fidelity = rung_fidelity(fidelity, all_rung)

    solution = jnp.zeros_like(all_targets)
    residual = all_targets
    direction = all_targets
    gram = outer_gram(residual, residual)
    for iteration in range(ITERS):
        image = (
            kernel_image(all_embedding, squares, all_rung, col_fidelity, inverse_scale, direction)
            + noise_var[0] * direction
        )
        curvature = outer_gram(direction, image)
        step_matrix = solve_spd(curvature, gram)
        solution = solution + jnp.dot(step_matrix.T, direction, precision=lax.Precision.HIGHEST)
        residual = residual - jnp.dot(step_matrix.T, image, precision=lax.Precision.HIGHEST)
        if iteration + 1 < ITERS:
            new_gram = outer_gram(residual, residual)
            update_matrix = solve_spd(gram, new_gram)
            direction = residual + jnp.dot(
                update_matrix.T, direction, precision=lax.Precision.HIGHEST
            )
            gram = new_gram
    own_solution = lax.dynamic_slice_in_dim(solution, own_first, own_count, 1)
    own_residual = lax.dynamic_slice_in_dim(residual, own_first, own_count, 1)
    return (own_solution, own_residual)


def solution(mesh):
    placed = (
        P(None, ("task", "row", "col")),
        P(("task", "row", "col")),
        P(),
        P(),
        P(),
        P(),
        P(),
        P(None, ("task", "row", "col")),
        P("task", None),
        P("task"),
        P("task"),
    )
    return jax.shard_map(
        on_device,
        mesh=mesh,
        in_specs=placed,
        out_specs=(P(None, ("task", "row", "col")), P(None, ("task", "row", "col"))),
        check_vma=False,
    )
```

```python
import jax
import jax.numpy as jnp
from jax import lax
from jax.sharding import PartitionSpec as P

ITERS = 2


def fidelity_matrix(fidelity_factor):
    lower = jnp.tril(fidelity_factor)
    return jnp.dot(lower, lower.T, precision=lax.Precision.HIGHEST) + 0.5 * jnp.eye(
        fidelity_factor.shape[0], dtype=jnp.float32
    )


def left_product(weights, values):
    return lax.dot_general(
        weights, values, (((0,), (0,)), ((), ())), preferred_element_type=jnp.float32
    )


def outer_gram(left_side, right_side):
    return lax.dot_general(
        left_side, right_side, (((1,), (1,)), ((), ())), precision=lax.Precision.HIGHEST
    )


def solve_spd(matrix, right_side):
    return jax.scipy.linalg.cho_solve((jnp.linalg.cholesky(matrix), True), right_side)


def block_size(total_count, largest):
    chosen = min(total_count, largest)
    while total_count % chosen != 0:
        chosen = chosen - 1
    return chosen


def rung_fidelity(fidelity, rung_value):
    levels = jnp.arange(fidelity.shape[0], dtype=jnp.float32)
    onehot = (rung_value.astype(jnp.float32)[None, :] == levels[:, None]).astype(jnp.float32)
    return jnp.dot(fidelity, onehot, precision=lax.Precision.HIGHEST)


def split_two(values):
    high = lax.reduce_precision(values, exponent_bits=8, mantissa_bits=7)
    return high.astype(jnp.bfloat16), (values - high).astype(jnp.bfloat16)


def split_product(direction, kernel):
    return pieces_product(direction, split_two(kernel))


def pieces_product(direction, pieces):
    count = direction.shape[0]
    d_high, d_low = split_two(direction)
    k_high, k_low = pieces
    dims = (((1,), (1,)), ((), ()))
    by_high = lax.dot_general(
        jnp.concatenate([d_high, d_low], axis=0), k_high, dims,
        preferred_element_type=jnp.float32,
    )
    by_low = lax.dot_general(d_high, k_low, dims, preferred_element_type=jnp.float32)
    return (by_high[:count] + by_high[count:]) + by_low


def whole_kernel_pieces(embedding, squares, rung_value, col_fidelity, inverse_scale):
    count = embedding.shape[1]
    if block_size(count, 2048) != count:
        return None
    direction = jnp.zeros((1, count), jnp.float32)
    (kernel,) = kernel_image(
        embedding, squares, rung_value, col_fidelity, inverse_scale, direction, whole=True
    )
    return lax.optimization_barrier(split_two(kernel))


def kernel_image(
    embedding, squares, rung_value, col_fidelity, inverse_scale, direction, whole=False
):
    count = embedding.shape[1]
    row_block = block_size(count, 2048)
    col_block = block_size(count, 2048)
    levels = jnp.arange(col_fidelity.shape[0], dtype=jnp.float32)

    def one_row_block(block_number):
        first_row = block_number * row_block
        rows_embedding = lax.dynamic_slice_in_dim(embedding, first_row, row_block, 1)
        rows_squares = lax.dynamic_slice_in_dim(squares, first_row, row_block, 0)
        rows_rung = lax.dynamic_slice_in_dim(rung_value, first_row, row_block, 0)
        rows_match = rows_rung.astype(jnp.float32)[:, None] == levels[None, :]

        def one_col_block(running, column_number):
            first_col = column_number * col_block
            cols_embedding = lax.dynamic_slice_in_dim(embedding, first_col, col_block, 1)
            cols_squares = lax.dynamic_slice_in_dim(squares, first_col, col_block, 0)
            cols_fidelity = lax.dynamic_slice_in_dim(col_fidelity, first_col, col_block, 1)
            cols_direction = lax.dynamic_slice_in_dim(direction, first_col, col_block, 1)
            inner = left_product(rows_embedding, cols_embedding)
            distance = rows_squares[:, None] + cols_squares[None, :] - 2.0 * inner
            tile_fidelity = cols_fidelity[0][None, :]
            for level in range(1, col_fidelity.shape[0]):
                tile_fidelity = jnp.where(
                    rows_match[:, level : level + 1], cols_fidelity[level][None, :], tile_fidelity
                )
            kernel = jnp.exp(-inverse_scale[0] * distance) * tile_fidelity
            if whole:
                return (running + (kernel,), None)
            contribution = split_product(cols_direction, kernel)
            return (running + contribution, None)

        if whole:
            result, unused = one_col_block((), 0)
            return result
        start_value = jnp.zeros((direction.shape[0], row_block), jnp.float32)
        result, unused = lax.scan(
            one_col_block, start_value, jnp.arange(count // col_block, dtype=jnp.int32)
        )
        return result

    if whole:
        return one_row_block(0)
    stacked = lax.map(one_row_block, jnp.arange(count // row_block, dtype=jnp.int32))
    return jnp.transpose(stacked, (1, 0, 2)).reshape(direction.shape[0], count)


def on_device(
    features,
    rung_index,
    w_first,
    b_first,
    w_second,
    b_second,
    w_third,
    targets,
    fidelity_factor,
    inverse_scale,
    noise_var,
):
    fidelity = fidelity_matrix(fidelity_factor)
    hidden_one = jax.nn.silu(left_product(w_first, features) + b_first[:, None]).astype(
        jnp.bfloat16
    )
    hidden_two = jax.nn.silu(left_product(w_second, hidden_one) + b_second[:, None]).astype(
        jnp.bfloat16
    )
    embedding = lax.reduce_precision(
        left_product(w_third, hidden_two), exponent_bits=8, mantissa_bits=7
    )
    rung_value = rung_index.astype(jnp.float32)
    own_count = targets.shape[1]
    own_first = (lax.axis_index("row") * lax.axis_size("col") + lax.axis_index("col")) * own_count

    emb_rows = embedding.shape[0]
    packed = jnp.concatenate(
        [embedding, targets, rung_value[None, :]], axis=0
    )
    gathered = lax.all_gather(packed, ("row", "col"), axis=1, tiled=True)
    all_embedding = gathered[:emb_rows].astype(jnp.bfloat16)
    all_targets = gathered[emb_rows : emb_rows + targets.shape[0]]
    all_rung = gathered[emb_rows + targets.shape[0]]

    squares = jnp.sum(jnp.square(gathered[:emb_rows]), axis=0)
    col_fidelity = rung_fidelity(fidelity, all_rung)

    pieces = whole_kernel_pieces(all_embedding, squares, all_rung, col_fidelity, inverse_scale)
    solution = jnp.zeros_like(all_targets)
    residual = all_targets
    direction = all_targets
    gram = outer_gram(residual, residual)
    for iteration in range(ITERS):
        if pieces is None:
            product = kernel_image(
                all_embedding, squares, all_rung, col_fidelity, inverse_scale, direction
            )
        else:
            product = pieces_product(direction, pieces)
        image = product + noise_var[0] * direction
        curvature = outer_gram(direction, image)
        step_matrix = solve_spd(curvature, gram)
        solution = solution + jnp.dot(step_matrix.T, direction, precision=lax.Precision.HIGHEST)
        residual = residual - jnp.dot(step_matrix.T, image, precision=lax.Precision.HIGHEST)
        if iteration + 1 < ITERS:
            new_gram = outer_gram(residual, residual)
            update_matrix = solve_spd(gram, new_gram)
            direction = residual + jnp.dot(
                update_matrix.T, direction, precision=lax.Precision.HIGHEST
            )
            gram = new_gram
    own_solution = lax.dynamic_slice_in_dim(solution, own_first, own_count, 1)
    own_residual = lax.dynamic_slice_in_dim(residual, own_first, own_count, 1)
    return (own_solution, own_residual)


def solution(mesh):
    placed = (
        P(None, ("task", "row", "col")),
        P(("task", "row", "col")),
        P(),
        P(),
        P(),
        P(),
        P(),
        P(None, ("task", "row", "col")),
        P("task", None),
        P("task"),
        P("task"),
    )
    return jax.shard_map(
        on_device,
        mesh=mesh,
        in_specs=placed,
        out_specs=(P(None, ("task", "row", "col")), P(None, ("task", "row", "col"))),
        check_vma=False,
    )
```

```python
import jax
import jax.numpy as jnp
from jax import lax
from jax.sharding import PartitionSpec as P
from jax.experimental import pallas as pl

ITERS = 2


def fidelity_matrix(fidelity_factor):
    lower = jnp.tril(fidelity_factor)
    return jnp.dot(lower, lower.T, precision=lax.Precision.HIGHEST) + 0.5 * jnp.eye(
        fidelity_factor.shape[0], dtype=jnp.float32
    )


def left_product(weights, values):
    return lax.dot_general(
        weights, values, (((0,), (0,)), ((), ())), preferred_element_type=jnp.float32
    )


def outer_gram(left_side, right_side):
    return lax.dot_general(
        left_side, right_side, (((1,), (1,)), ((), ())), precision=lax.Precision.HIGHEST
    )


def solve_spd(matrix, right_side):
    return jax.scipy.linalg.cho_solve((jnp.linalg.cholesky(matrix), True), right_side)


def block_size(total_count, largest):
    chosen = min(total_count, largest)
    while total_count % chosen != 0:
        chosen = chosen - 1
    return chosen


def rung_fidelity(fidelity, rung_value):
    levels = jnp.arange(fidelity.shape[0], dtype=jnp.float32)
    onehot = (rung_value.astype(jnp.float32)[None, :] == levels[:, None]).astype(jnp.float32)
    return jnp.dot(fidelity, onehot, precision=lax.Precision.HIGHEST)


def split_two(values):
    high = lax.reduce_precision(values, exponent_bits=8, mantissa_bits=7)
    return high.astype(jnp.bfloat16), (values - high).astype(jnp.bfloat16)


def split_product(direction, kernel):
    count = direction.shape[0]
    d_high, d_low = split_two(direction)
    k_high, k_low = split_two(kernel)
    dims = (((1,), (1,)), ((), ()))
    by_high = lax.dot_general(
        jnp.concatenate([d_high, d_low], axis=0), k_high, dims,
        preferred_element_type=jnp.float32,
    )
    by_low = lax.dot_general(d_high, k_low, dims, preferred_element_type=jnp.float32)
    return (by_high[:count] + by_high[count:]) + by_low


def kernel_image(embedding, squares, rung_value, col_fidelity, inverse_scale, direction):
    count = embedding.shape[1]
    row_block = block_size(count, 2048)
    col_block = block_size(count, 2048)
    levels = jnp.arange(col_fidelity.shape[0], dtype=jnp.float32)

    def one_row_block(block_number):
        first_row = block_number * row_block
        rows_embedding = lax.dynamic_slice_in_dim(embedding, first_row, row_block, 1)
        rows_squares = lax.dynamic_slice_in_dim(squares, first_row, row_block, 0)
        rows_rung = lax.dynamic_slice_in_dim(rung_value, first_row, row_block, 0)
        rows_match = rows_rung.astype(jnp.float32)[:, None] == levels[None, :]

        def one_col_block(running, column_number):
            first_col = column_number * col_block
            cols_embedding = lax.dynamic_slice_in_dim(embedding, first_col, col_block, 1)
            cols_squares = lax.dynamic_slice_in_dim(squares, first_col, col_block, 0)
            cols_fidelity = lax.dynamic_slice_in_dim(col_fidelity, first_col, col_block, 1)
            cols_direction = lax.dynamic_slice_in_dim(direction, first_col, col_block, 1)
            inner = left_product(rows_embedding, cols_embedding)
            distance = rows_squares[:, None] + cols_squares[None, :] - 2.0 * inner
            tile_fidelity = cols_fidelity[0][None, :]
            for level in range(1, col_fidelity.shape[0]):
                tile_fidelity = jnp.where(
                    rows_match[:, level : level + 1], cols_fidelity[level][None, :], tile_fidelity
                )
            kernel = jnp.exp(-inverse_scale[0] * distance) * tile_fidelity
            contribution = split_product(cols_direction, kernel)
            return (running + contribution, None)

        start_value = jnp.zeros((direction.shape[0], row_block), jnp.float32)
        result, unused = lax.scan(
            one_col_block, start_value, jnp.arange(count // col_block, dtype=jnp.int32)
        )
        return result

    stacked = lax.map(one_row_block, jnp.arange(count // row_block, dtype=jnp.int32))
    return jnp.transpose(stacked, (1, 0, 2)).reshape(direction.shape[0], count)


def embed_block(
    features_ref, w_first_ref, b_first_ref, w_second_ref, b_second_ref, w_third_ref,
    targets_ref, rung_ref, out_ref,
):
    dims = (((0,), (0,)), ((), ()))
    first = lax.dot_general(
        w_first_ref[...], features_ref[...], dims, preferred_element_type=jnp.float32
    )
    hidden_one = jax.nn.silu(first + b_first_ref[...]).astype(jnp.bfloat16)
    second = lax.dot_general(
        w_second_ref[...], hidden_one, dims, preferred_element_type=jnp.float32
    )
    hidden_two = jax.nn.silu(second + b_second_ref[...]).astype(jnp.bfloat16)
    embedding = lax.dot_general(
        w_third_ref[...], hidden_two, dims, preferred_element_type=jnp.float32
    )
    emb_rows = embedding.shape[0]
    rhs = targets_ref.shape[0]
    out_ref[:emb_rows, :] = embedding.astype(jnp.bfloat16).astype(jnp.float32)
    out_ref[emb_rows : emb_rows + rhs, :] = targets_ref[...]
    out_ref[emb_rows + rhs :, :] = rung_ref[...]


def on_device(
    features,
    rung_index,
    w_first,
    b_first,
    w_second,
    b_second,
    w_third,
    targets,
    fidelity_factor,
    inverse_scale,
    noise_var,
):
    fidelity = fidelity_matrix(fidelity_factor)
    emb_rows = w_third.shape[1]
    own_count = targets.shape[1]
    own_first = (lax.axis_index("row") * lax.axis_size("col") + lax.axis_index("col")) * own_count
    packed = pl.pallas_call(
        embed_block,
        out_shape=jax.ShapeDtypeStruct(
            (emb_rows + targets.shape[0] + 1, own_count), jnp.float32
        ),
    )(
        features,
        w_first,
        b_first[:, None],
        w_second,
        b_second[:, None],
        w_third,
        targets,
        rung_index.astype(jnp.float32)[None, :],
    )
    gathered = lax.all_gather(packed, ("row", "col"), axis=1, tiled=True)
    all_embedding = gathered[:emb_rows].astype(jnp.bfloat16)
    all_targets = gathered[emb_rows : emb_rows + targets.shape[0]]
    all_rung = gathered[emb_rows + targets.shape[0]]

    squares = jnp.sum(jnp.square(gathered[:emb_rows]), axis=0)
    col_fidelity = rung_fidelity(fidelity, all_rung)

    solution = jnp.zeros_like(all_targets)
    residual = all_targets
    direction = all_targets
    gram = outer_gram(residual, residual)
    for iteration in range(ITERS):
        image = (
            kernel_image(all_embedding, squares, all_rung, col_fidelity, inverse_scale, direction)
            + noise_var[0] * direction
        )
        curvature = outer_gram(direction, image)
        step_matrix = solve_spd(curvature, gram)
        solution = solution + jnp.dot(step_matrix.T, direction, precision=lax.Precision.HIGHEST)
        residual = residual - jnp.dot(step_matrix.T, image, precision=lax.Precision.HIGHEST)
        if iteration + 1 < ITERS:
            new_gram = outer_gram(residual, residual)
            update_matrix = solve_spd(gram, new_gram)
            direction = residual + jnp.dot(
                update_matrix.T, direction, precision=lax.Precision.HIGHEST
            )
            gram = new_gram
    own_solution = lax.dynamic_slice_in_dim(solution, own_first, own_count, 1)
    own_residual = lax.dynamic_slice_in_dim(residual, own_first, own_count, 1)
    return (own_solution, own_residual)


def solution(mesh):
    placed = (
        P(None, ("task", "row", "col")),
        P(("task", "row", "col")),
        P(),
        P(),
        P(),
        P(),
        P(),
        P(None, ("task", "row", "col")),
        P("task", None),
        P("task"),
        P("task"),
    )
    return jax.shard_map(
        on_device,
        mesh=mesh,
        in_specs=placed,
        out_specs=(P(None, ("task", "row", "col")), P(None, ("task", "row", "col"))),
        check_vma=False,
    )
```

```python
import jax
import jax.numpy as jnp
from jax import lax
from jax.sharding import PartitionSpec as P

ITERS = 2


def fidelity_matrix(fidelity_factor):
    lower = jnp.tril(fidelity_factor)
    return jnp.dot(lower, lower.T, precision=lax.Precision.HIGHEST) + 0.5 * jnp.eye(
        fidelity_factor.shape[0], dtype=jnp.float32
    )


def left_product(weights, values):
    return lax.dot_general(
        weights, values, (((0,), (0,)), ((), ())), preferred_element_type=jnp.float32
    )


def outer_gram(left_side, right_side):
    return lax.dot_general(
        left_side, right_side, (((1,), (1,)), ((), ())), precision=lax.Precision.HIGHEST
    )


def solve_spd(matrix, right_side):
    return jax.scipy.linalg.cho_solve((jnp.linalg.cholesky(matrix), True), right_side)


def block_size(total_count, largest):
    chosen = min(total_count, largest)
    while total_count % chosen != 0:
        chosen = chosen - 1
    return chosen


def rung_fidelity(fidelity, rung_value):
    levels = jnp.arange(fidelity.shape[0], dtype=jnp.float32)
    onehot = (rung_value.astype(jnp.float32)[None, :] == levels[:, None]).astype(jnp.float32)
    return jnp.dot(fidelity, onehot, precision=lax.Precision.HIGHEST)


def split_two(values):
    high = lax.reduce_precision(values, exponent_bits=8, mantissa_bits=7)
    return high.astype(jnp.bfloat16), (values - high).astype(jnp.bfloat16)


def split_product(direction, kernel):
    count = direction.shape[0]
    d_high, d_low = split_two(direction)
    k_high, k_low = split_two(kernel)
    dims = (((1,), (1,)), ((), ()))
    by_high = lax.dot_general(
        jnp.concatenate([d_high, d_low], axis=0), k_high, dims,
        preferred_element_type=jnp.float32,
    )
    by_low = lax.dot_general(d_high, k_low, dims, preferred_element_type=jnp.float32)
    return (by_high[:count] + by_high[count:]) + by_low


def kernel_image(embedding, squares, rung_value, col_fidelity, inverse_scale, direction):
    count = embedding.shape[1]
    row_block = block_size(count, 2048)
    col_block = block_size(count, 2048)
    levels = jnp.arange(col_fidelity.shape[0], dtype=jnp.float32)

    def one_row_block(block_number):
        first_row = block_number * row_block
        rows_embedding = lax.dynamic_slice_in_dim(embedding, first_row, row_block, 1)
        rows_squares = lax.dynamic_slice_in_dim(squares, first_row, row_block, 0)
        rows_rung = lax.dynamic_slice_in_dim(rung_value, first_row, row_block, 0)
        rows_fidelity = lax.dynamic_slice_in_dim(col_fidelity, first_row, row_block, 1)

        def one_col_block(running, column_number):
            first_col = column_number * col_block
            cols_embedding = lax.dynamic_slice_in_dim(embedding, first_col, col_block, 1)
            cols_squares = lax.dynamic_slice_in_dim(squares, first_col, col_block, 0)
            cols_fidelity = lax.dynamic_slice_in_dim(col_fidelity, first_col, col_block, 1)
            cols_direction = lax.dynamic_slice_in_dim(direction, first_col, col_block, 1)
            cols_rung = lax.dynamic_slice_in_dim(rung_value, first_col, col_block, 0)
            inner = left_product(rows_embedding, cols_embedding)
            distance = rows_squares[:, None] + cols_squares[None, :] - 2.0 * inner
            radial = jnp.exp(-inverse_scale[0] * distance)
            by_rung = jnp.concatenate(
                [
                    jnp.where(cols_rung[None, :] == levels[level], cols_direction, 0.0)
                    for level in range(col_fidelity.shape[0])
                ],
                axis=0,
            )
            rung_products = split_product(by_rung, radial)
            rhs = direction.shape[0]
            contribution = rows_fidelity[0][None, :] * rung_products[:rhs]
            for level in range(1, col_fidelity.shape[0]):
                contribution = contribution + rows_fidelity[level][None, :] * rung_products[
                    level * rhs : (level + 1) * rhs
                ]
            return (running + contribution, None)

        start_value = jnp.zeros((direction.shape[0], row_block), jnp.float32)
        result, unused = lax.scan(
            one_col_block, start_value, jnp.arange(count // col_block, dtype=jnp.int32)
        )
        return result

    stacked = lax.map(one_row_block, jnp.arange(count // row_block, dtype=jnp.int32))
    return jnp.transpose(stacked, (1, 0, 2)).reshape(direction.shape[0], count)


def on_device(
    features,
    rung_index,
    w_first,
    b_first,
    w_second,
    b_second,
    w_third,
    targets,
    fidelity_factor,
    inverse_scale,
    noise_var,
):
    fidelity = fidelity_matrix(fidelity_factor)
    hidden_one = jax.nn.silu(left_product(w_first, features) + b_first[:, None]).astype(
        jnp.bfloat16
    )
    hidden_two = jax.nn.silu(left_product(w_second, hidden_one) + b_second[:, None]).astype(
        jnp.bfloat16
    )
    embedding = lax.reduce_precision(
        left_product(w_third, hidden_two), exponent_bits=8, mantissa_bits=7
    )
    rung_value = rung_index.astype(jnp.float32)
    own_count = targets.shape[1]
    own_first = (lax.axis_index("row") * lax.axis_size("col") + lax.axis_index("col")) * own_count

    emb_rows = embedding.shape[0]
    packed = jnp.concatenate(
        [embedding, targets, rung_value[None, :]], axis=0
    )
    gathered = lax.all_gather(packed, ("row", "col"), axis=1, tiled=True)
    all_embedding = gathered[:emb_rows].astype(jnp.bfloat16)
    all_targets = gathered[emb_rows : emb_rows + targets.shape[0]]
    all_rung = gathered[emb_rows + targets.shape[0]]

    squares = jnp.sum(jnp.square(gathered[:emb_rows]), axis=0)
    col_fidelity = rung_fidelity(fidelity, all_rung)

    solution = jnp.zeros_like(all_targets)
    residual = all_targets
    direction = all_targets
    gram = outer_gram(residual, residual)
    for iteration in range(ITERS):
        image = (
            kernel_image(all_embedding, squares, all_rung, col_fidelity, inverse_scale, direction)
            + noise_var[0] * direction
        )
        curvature = outer_gram(direction, image)
        step_matrix = solve_spd(curvature, gram)
        solution = solution + jnp.dot(step_matrix.T, direction, precision=lax.Precision.HIGHEST)
        residual = residual - jnp.dot(step_matrix.T, image, precision=lax.Precision.HIGHEST)
        if iteration + 1 < ITERS:
            new_gram = outer_gram(residual, residual)
            update_matrix = solve_spd(gram, new_gram)
            direction = residual + jnp.dot(
                update_matrix.T, direction, precision=lax.Precision.HIGHEST
            )
            gram = new_gram
    own_solution = lax.dynamic_slice_in_dim(solution, own_first, own_count, 1)
    own_residual = lax.dynamic_slice_in_dim(residual, own_first, own_count, 1)
    return (own_solution, own_residual)


def solution(mesh):
    placed = (
        P(None, ("task", "row", "col")),
        P(("task", "row", "col")),
        P(),
        P(),
        P(),
        P(),
        P(),
        P(None, ("task", "row", "col")),
        P("task", None),
        P("task"),
        P("task"),
    )
    return jax.shard_map(
        on_device,
        mesh=mesh,
        in_specs=placed,
        out_specs=(P(None, ("task", "row", "col")), P(None, ("task", "row", "col"))),
        check_vma=False,
    )
```

```python
import jax
import jax.numpy as jnp
from jax import lax
from jax.sharding import PartitionSpec as P

ITERS = 2


def fidelity_matrix(fidelity_factor):
    lower = jnp.tril(fidelity_factor)
    return jnp.dot(lower, lower.T, precision=lax.Precision.HIGHEST) + 0.5 * jnp.eye(
        fidelity_factor.shape[0], dtype=jnp.float32
    )


def left_product(weights, values):
    return lax.dot_general(
        weights, values, (((0,), (0,)), ((), ())), preferred_element_type=jnp.float32
    )


def outer_gram(left_side, right_side):
    return lax.dot_general(
        left_side, right_side, (((1,), (1,)), ((), ())), precision=lax.Precision.HIGHEST
    )


def solve_spd(matrix, right_side):
    return jax.scipy.linalg.cho_solve((jnp.linalg.cholesky(matrix), True), right_side)


def block_size(total_count, largest):
    chosen = min(total_count, largest)
    while total_count % chosen != 0:
        chosen = chosen - 1
    return chosen


def rung_fidelity(fidelity, rung_value):
    levels = jnp.arange(fidelity.shape[0], dtype=jnp.float32)
    onehot = (rung_value.astype(jnp.float32)[None, :] == levels[:, None]).astype(jnp.float32)
    return jnp.dot(fidelity, onehot, precision=lax.Precision.HIGHEST), onehot


def split_two(values):
    high = lax.reduce_precision(values, exponent_bits=8, mantissa_bits=7)
    return high.astype(jnp.bfloat16), (values - high).astype(jnp.bfloat16)


def split_product(direction, kernel):
    count = direction.shape[0]
    d_high, d_low = split_two(direction)
    k_high, k_low = split_two(kernel)
    dims = (((1,), (1,)), ((), ()))
    by_high = lax.dot_general(
        jnp.concatenate([d_high, d_low], axis=0), k_high, dims,
        preferred_element_type=jnp.float32,
    )
    by_low = lax.dot_general(d_high, k_low, dims, preferred_element_type=jnp.float32)
    return (by_high[:count] + by_high[count:]) + by_low


def kernel_image(embedding, squares, rung_onehot, col_fidelity, inverse_scale, direction):
    count = embedding.shape[1]
    row_block = block_size(count, 2048)
    col_block = block_size(count, 2048)
    levels = jnp.arange(col_fidelity.shape[0], dtype=jnp.float32)

    def one_row_block(block_number):
        first_row = block_number * row_block
        rows_embedding = lax.dynamic_slice_in_dim(embedding, first_row, row_block, 1)
        rows_squares = lax.dynamic_slice_in_dim(squares, first_row, row_block, 0)
        rows_fidelity = lax.dynamic_slice_in_dim(col_fidelity, first_row, row_block, 1)

        def one_col_block(running, column_number):
            first_col = column_number * col_block
            cols_embedding = lax.dynamic_slice_in_dim(embedding, first_col, col_block, 1)
            cols_squares = lax.dynamic_slice_in_dim(squares, first_col, col_block, 0)
            cols_fidelity = lax.dynamic_slice_in_dim(col_fidelity, first_col, col_block, 1)
            cols_direction = lax.dynamic_slice_in_dim(direction, first_col, col_block, 1)
            cols_onehot = lax.dynamic_slice_in_dim(rung_onehot, first_col, col_block, 1)
            inner = left_product(rows_embedding, cols_embedding)
            distance = rows_squares[:, None] + cols_squares[None, :] - 2.0 * inner
            radial = jnp.exp(-inverse_scale[0] * distance)
            by_rung = jnp.concatenate(
                [
                    cols_direction * cols_onehot[level][None, :]
                    for level in range(col_fidelity.shape[0])
                ],
                axis=0,
            )
            rung_products = split_product(by_rung, radial)
            rhs = direction.shape[0]
            contribution = rows_fidelity[0][None, :] * rung_products[:rhs]
            for level in range(1, col_fidelity.shape[0]):
                contribution = contribution + rows_fidelity[level][None, :] * rung_products[
                    level * rhs : (level + 1) * rhs
                ]
            return (running + contribution, None)

        start_value = jnp.zeros((direction.shape[0], row_block), jnp.float32)
        result, unused = lax.scan(
            one_col_block, start_value, jnp.arange(count // col_block, dtype=jnp.int32)
        )
        return result

    stacked = lax.map(one_row_block, jnp.arange(count // row_block, dtype=jnp.int32))
    return jnp.transpose(stacked, (1, 0, 2)).reshape(direction.shape[0], count)


def on_device(
    features,
    rung_index,
    w_first,
    b_first,
    w_second,
    b_second,
    w_third,
    targets,
    fidelity_factor,
    inverse_scale,
    noise_var,
):
    fidelity = fidelity_matrix(fidelity_factor)
    hidden_one = jax.nn.silu(left_product(w_first, features) + b_first[:, None]).astype(
        jnp.bfloat16
    )
    hidden_two = jax.nn.silu(left_product(w_second, hidden_one) + b_second[:, None]).astype(
        jnp.bfloat16
    )
    embedding = lax.reduce_precision(
        left_product(w_third, hidden_two), exponent_bits=8, mantissa_bits=7
    )
    rung_value = rung_index.astype(jnp.float32)
    own_count = targets.shape[1]
    own_first = (lax.axis_index("row") * lax.axis_size("col") + lax.axis_index("col")) * own_count

    emb_rows = embedding.shape[0]
    packed = jnp.concatenate(
        [embedding, targets, rung_value[None, :]], axis=0
    )
    gathered = lax.all_gather(packed, ("row", "col"), axis=1, tiled=True)
    all_embedding = gathered[:emb_rows].astype(jnp.bfloat16)
    all_targets = gathered[emb_rows : emb_rows + targets.shape[0]]
    all_rung = gathered[emb_rows + targets.shape[0]]

    squares = jnp.sum(jnp.square(gathered[:emb_rows]), axis=0)
    col_fidelity, rung_onehot = rung_fidelity(fidelity, all_rung)

    solution = jnp.zeros_like(all_targets)
    residual = all_targets
    direction = all_targets
    gram = outer_gram(residual, residual)
    for iteration in range(ITERS):
        image = (
            kernel_image(all_embedding, squares, rung_onehot, col_fidelity, inverse_scale, direction)
            + noise_var[0] * direction
        )
        curvature = outer_gram(direction, image)
        step_matrix = solve_spd(curvature, gram)
        solution = solution + jnp.dot(step_matrix.T, direction, precision=lax.Precision.HIGHEST)
        residual = residual - jnp.dot(step_matrix.T, image, precision=lax.Precision.HIGHEST)
        if iteration + 1 < ITERS:
            new_gram = outer_gram(residual, residual)
            update_matrix = solve_spd(gram, new_gram)
            direction = residual + jnp.dot(
                update_matrix.T, direction, precision=lax.Precision.HIGHEST
            )
            gram = new_gram
    own_solution = lax.dynamic_slice_in_dim(solution, own_first, own_count, 1)
    own_residual = lax.dynamic_slice_in_dim(residual, own_first, own_count, 1)
    return (own_solution, own_residual)


def solution(mesh):
    placed = (
        P(None, ("task", "row", "col")),
        P(("task", "row", "col")),
        P(),
        P(),
        P(),
        P(),
        P(),
        P(None, ("task", "row", "col")),
        P("task", None),
        P("task"),
        P("task"),
    )
    return jax.shard_map(
        on_device,
        mesh=mesh,
        in_specs=placed,
        out_specs=(P(None, ("task", "row", "col")), P(None, ("task", "row", "col"))),
        check_vma=False,
    )
```

```python
import jax
import jax.numpy as jnp
from jax import lax
from jax.sharding import PartitionSpec as P

ITERS = 2


def fidelity_matrix(fidelity_factor):
    lower = jnp.tril(fidelity_factor)
    return jnp.dot(lower, lower.T, precision=lax.Precision.HIGHEST) + 0.5 * jnp.eye(
        fidelity_factor.shape[0], dtype=jnp.float32
    )


def left_product(weights, values):
    return lax.dot_general(
        weights, values, (((0,), (0,)), ((), ())), preferred_element_type=jnp.float32
    )


def outer_gram(left_side, right_side):
    return lax.dot_general(
        left_side, right_side, (((1,), (1,)), ((), ())), precision=lax.Precision.HIGHEST
    )


def solve_spd(matrix, right_side):
    return jax.scipy.linalg.cho_solve((jnp.linalg.cholesky(matrix), True), right_side)


def block_size(total_count, largest):
    chosen = min(total_count, largest)
    while total_count % chosen != 0:
        chosen = chosen - 1
    return chosen


def rung_fidelity(fidelity, rung_value):
    levels = jnp.arange(fidelity.shape[0], dtype=jnp.float32)
    onehot = (rung_value.astype(jnp.float32)[None, :] == levels[:, None]).astype(jnp.float32)
    return jnp.dot(fidelity, onehot, precision=lax.Precision.HIGHEST), onehot


def split_two(values):
    high = lax.reduce_precision(values, exponent_bits=8, mantissa_bits=7)
    return high.astype(jnp.bfloat16), (values - high).astype(jnp.bfloat16)


def split_product(direction, kernel):
    return pieces_product(direction, split_two(kernel))


def pieces_product(direction, pieces):
    count = direction.shape[0]
    d_high, d_low = split_two(direction)
    k_high, k_low = pieces
    dims = (((1,), (1,)), ((), ()))
    by_high = lax.dot_general(
        jnp.concatenate([d_high, d_low], axis=0), k_high, dims,
        preferred_element_type=jnp.float32,
    )
    by_low = lax.dot_general(d_high, k_low, dims, preferred_element_type=jnp.float32)
    return (by_high[:count] + by_high[count:]) + by_low


def whole_radial_pieces(embedding, squares, inverse_scale):
    count = embedding.shape[1]
    if block_size(count, 2048) != count:
        return None
    inner = left_product(embedding, embedding)
    distance = squares[:, None] + squares[None, :] - 2.0 * inner
    radial = jnp.exp(-inverse_scale[0] * distance)
    return lax.optimization_barrier(split_two(radial))


def kernel_image(
    embedding, squares, rung_onehot, col_fidelity, inverse_scale, direction, pieces=None
):
    count = embedding.shape[1]
    row_block = block_size(count, 2048)
    col_block = block_size(count, 2048)
    levels = jnp.arange(col_fidelity.shape[0], dtype=jnp.float32)

    def one_row_block(block_number):
        first_row = block_number * row_block
        rows_embedding = lax.dynamic_slice_in_dim(embedding, first_row, row_block, 1)
        rows_squares = lax.dynamic_slice_in_dim(squares, first_row, row_block, 0)
        rows_fidelity = lax.dynamic_slice_in_dim(col_fidelity, first_row, row_block, 1)

        def one_col_block(running, column_number):
            first_col = column_number * col_block
            cols_embedding = lax.dynamic_slice_in_dim(embedding, first_col, col_block, 1)
            cols_squares = lax.dynamic_slice_in_dim(squares, first_col, col_block, 0)
            cols_fidelity = lax.dynamic_slice_in_dim(col_fidelity, first_col, col_block, 1)
            cols_direction = lax.dynamic_slice_in_dim(direction, first_col, col_block, 1)
            cols_onehot = lax.dynamic_slice_in_dim(rung_onehot, first_col, col_block, 1)
            if pieces is None:
                inner = left_product(rows_embedding, cols_embedding)
                distance = rows_squares[:, None] + cols_squares[None, :] - 2.0 * inner
                radial_pieces = split_two(jnp.exp(-inverse_scale[0] * distance))
            else:
                radial_pieces = pieces
            by_rung = jnp.concatenate(
                [
                    cols_direction * cols_onehot[level][None, :]
                    for level in range(col_fidelity.shape[0])
                ],
                axis=0,
            )
            rung_products = pieces_product(by_rung, radial_pieces)
            rhs = direction.shape[0]
            contribution = rows_fidelity[0][None, :] * rung_products[:rhs]
            for level in range(1, col_fidelity.shape[0]):
                contribution = contribution + rows_fidelity[level][None, :] * rung_products[
                    level * rhs : (level + 1) * rhs
                ]
            return (running + contribution, None)

        start_value = jnp.zeros((direction.shape[0], row_block), jnp.float32)
        result, unused = lax.scan(
            one_col_block, start_value, jnp.arange(count // col_block, dtype=jnp.int32)
        )
        return result

    stacked = lax.map(one_row_block, jnp.arange(count // row_block, dtype=jnp.int32))
    return jnp.transpose(stacked, (1, 0, 2)).reshape(direction.shape[0], count)


def on_device(
    features,
    rung_index,
    w_first,
    b_first,
    w_second,
    b_second,
    w_third,
    targets,
    fidelity_factor,
    inverse_scale,
    noise_var,
):
    fidelity = fidelity_matrix(fidelity_factor)
    hidden_one = jax.nn.silu(left_product(w_first, features) + b_first[:, None]).astype(
        jnp.bfloat16
    )
    hidden_two = jax.nn.silu(left_product(w_second, hidden_one) + b_second[:, None]).astype(
        jnp.bfloat16
    )
    embedding = lax.reduce_precision(
        left_product(w_third, hidden_two), exponent_bits=8, mantissa_bits=7
    )
    rung_value = rung_index.astype(jnp.float32)
    own_count = targets.shape[1]
    own_first = (lax.axis_index("row") * lax.axis_size("col") + lax.axis_index("col")) * own_count

    emb_rows = embedding.shape[0]
    packed = jnp.concatenate(
        [embedding, targets, rung_value[None, :]], axis=0
    )
    gathered = lax.all_gather(packed, ("row", "col"), axis=1, tiled=True)
    all_embedding = gathered[:emb_rows].astype(jnp.bfloat16)
    all_targets = gathered[emb_rows : emb_rows + targets.shape[0]]
    all_rung = gathered[emb_rows + targets.shape[0]]

    squares = jnp.sum(jnp.square(gathered[:emb_rows]), axis=0)
    col_fidelity, rung_onehot = rung_fidelity(fidelity, all_rung)

    pieces = whole_radial_pieces(all_embedding, squares, inverse_scale)
    solution = jnp.zeros_like(all_targets)
    residual = all_targets
    direction = all_targets
    gram = outer_gram(residual, residual)
    for iteration in range(ITERS):
        image = (
            kernel_image(
                all_embedding, squares, rung_onehot, col_fidelity, inverse_scale, direction,
                pieces,
            )
            + noise_var[0] * direction
        )
        curvature = outer_gram(direction, image)
        step_matrix = solve_spd(curvature, gram)
        solution = solution + jnp.dot(step_matrix.T, direction, precision=lax.Precision.HIGHEST)
        residual = residual - jnp.dot(step_matrix.T, image, precision=lax.Precision.HIGHEST)
        if iteration + 1 < ITERS:
            new_gram = outer_gram(residual, residual)
            update_matrix = solve_spd(gram, new_gram)
            direction = residual + jnp.dot(
                update_matrix.T, direction, precision=lax.Precision.HIGHEST
            )
            gram = new_gram
    own_solution = lax.dynamic_slice_in_dim(solution, own_first, own_count, 1)
    own_residual = lax.dynamic_slice_in_dim(residual, own_first, own_count, 1)
    return (own_solution, own_residual)


def solution(mesh):
    placed = (
        P(None, ("task", "row", "col")),
        P(("task", "row", "col")),
        P(),
        P(),
        P(),
        P(),
        P(),
        P(None, ("task", "row", "col")),
        P("task", None),
        P("task"),
        P("task"),
    )
    return jax.shard_map(
        on_device,
        mesh=mesh,
        in_specs=placed,
        out_specs=(P(None, ("task", "row", "col")), P(None, ("task", "row", "col"))),
        check_vma=False,
    )
```

```python
import jax
import jax.numpy as jnp
from jax import lax
from jax.sharding import PartitionSpec as P

ITERS = 2


def fidelity_matrix(fidelity_factor):
    lower = jnp.tril(fidelity_factor)
    return jnp.dot(lower, lower.T, precision=lax.Precision.HIGHEST) + 0.5 * jnp.eye(
        fidelity_factor.shape[0], dtype=jnp.float32
    )


def left_product(weights, values):
    return lax.dot_general(
        weights, values, (((0,), (0,)), ((), ())), preferred_element_type=jnp.float32
    )


def outer_gram(left_side, right_side):
    return lax.dot_general(
        left_side, right_side, (((1,), (1,)), ((), ())), precision=lax.Precision.HIGHEST
    )


def solve_spd(matrix, right_side):
    return jax.scipy.linalg.cho_solve((jnp.linalg.cholesky(matrix), True), right_side)


def block_size(total_count, largest):
    chosen = min(total_count, largest)
    while total_count % chosen != 0:
        chosen = chosen - 1
    return chosen


def rung_fidelity(fidelity, rung_value):
    levels = jnp.arange(fidelity.shape[0], dtype=jnp.float32)
    onehot = (rung_value.astype(jnp.float32)[None, :] == levels[:, None]).astype(jnp.float32)
    return jnp.dot(fidelity, onehot, precision=lax.Precision.HIGHEST), onehot


def split_two(values):
    high = lax.reduce_precision(values, exponent_bits=8, mantissa_bits=7)
    return high.astype(jnp.bfloat16), (values - high).astype(jnp.bfloat16)


def split_product(direction, kernel):
    return pieces_product(direction, split_two(kernel))


def pieces_product(direction, pieces):
    count = direction.shape[0]
    d_high, d_low = split_two(direction)
    k_high, k_low = pieces
    dims = (((1,), (1,)), ((), ()))
    by_high = lax.dot_general(
        jnp.concatenate([d_high, d_low], axis=0), k_high, dims,
        preferred_element_type=jnp.float32,
    )
    by_low = lax.dot_general(d_high, k_low, dims, preferred_element_type=jnp.float32)
    return (by_high[:count] + by_high[count:]) + by_low


def whole_radial_pieces(embedding, squares, inverse_scale):
    count = embedding.shape[1]
    if block_size(count, 2048) != count:
        return None
    inner = left_product(embedding, embedding)
    distance = squares[:, None] + squares[None, :] - 2.0 * inner
    radial = jnp.exp(-inverse_scale[0] * distance)
    return lax.optimization_barrier(split_two(radial))


def kernel_image(
    embedding, squares, rung_onehot, col_fidelity, inverse_scale, direction, pieces=None
):
    count = embedding.shape[1]
    row_block = block_size(count, 2048)
    col_block = block_size(count, 2048)
    levels = jnp.arange(col_fidelity.shape[0], dtype=jnp.float32)

    def one_row_block(block_number):
        first_row = block_number * row_block
        rows_embedding = lax.dynamic_slice_in_dim(embedding, first_row, row_block, 1)
        rows_squares = lax.dynamic_slice_in_dim(squares, first_row, row_block, 0)
        rows_fidelity = lax.dynamic_slice_in_dim(col_fidelity, first_row, row_block, 1)

        def one_col_block(running, column_number):
            first_col = column_number * col_block
            cols_embedding = lax.dynamic_slice_in_dim(embedding, first_col, col_block, 1)
            cols_squares = lax.dynamic_slice_in_dim(squares, first_col, col_block, 0)
            cols_fidelity = lax.dynamic_slice_in_dim(col_fidelity, first_col, col_block, 1)
            cols_direction = lax.dynamic_slice_in_dim(direction, first_col, col_block, 1)
            cols_onehot = lax.dynamic_slice_in_dim(rung_onehot, first_col, col_block, 1)
            if pieces is None:
                inner = left_product(rows_embedding, cols_embedding)
                distance = rows_squares[:, None] + cols_squares[None, :] - 2.0 * inner
                radial_pieces = split_two(jnp.exp(-inverse_scale[0] * distance))
            else:
                radial_pieces = pieces
            by_rung = jnp.concatenate(
                [
                    cols_direction * cols_onehot[level][None, :]
                    for level in range(col_fidelity.shape[0])
                ],
                axis=0,
            )
            rung_products = pieces_product(by_rung, radial_pieces)
            rhs = direction.shape[0]
            contribution = rows_fidelity[0][None, :] * rung_products[:rhs]
            for level in range(1, col_fidelity.shape[0]):
                contribution = contribution + rows_fidelity[level][None, :] * rung_products[
                    level * rhs : (level + 1) * rhs
                ]
            return (running + contribution, None)

        start_value = jnp.zeros((direction.shape[0], row_block), jnp.float32)
        result, unused = lax.scan(
            one_col_block, start_value, jnp.arange(count // col_block, dtype=jnp.int32)
        )
        return result

    stacked = lax.map(one_row_block, jnp.arange(count // row_block, dtype=jnp.int32))
    return jnp.transpose(stacked, (1, 0, 2)).reshape(direction.shape[0], count)


def on_device(
    features,
    rung_index,
    w_first,
    b_first,
    w_second,
    b_second,
    w_third,
    targets,
    fidelity_factor,
    inverse_scale,
    noise_var,
):
    fidelity = fidelity_matrix(fidelity_factor)
    hidden_one = jax.nn.silu(left_product(w_first, features) + b_first[:, None]).astype(
        jnp.bfloat16
    )
    hidden_two = jax.nn.silu(left_product(w_second, hidden_one) + b_second[:, None]).astype(
        jnp.bfloat16
    )
    embedding = lax.reduce_precision(
        left_product(w_third, hidden_two), exponent_bits=8, mantissa_bits=7
    )
    rung_value = rung_index.astype(jnp.float32)
    own_count = targets.shape[1]
    own_first = (lax.axis_index("row") * lax.axis_size("col") + lax.axis_index("col")) * own_count

    emb_rows = embedding.shape[0]
    packed = jnp.concatenate(
        [embedding, targets, rung_value[None, :]], axis=0
    )
    gathered = lax.all_gather(packed, ("row", "col"), axis=1, tiled=True)
    all_embedding = gathered[:emb_rows].astype(jnp.bfloat16)
    all_targets = gathered[emb_rows : emb_rows + targets.shape[0]]
    all_rung = gathered[emb_rows + targets.shape[0]]

    squares = jnp.sum(jnp.square(gathered[:emb_rows]), axis=0)
    col_fidelity, rung_onehot = rung_fidelity(fidelity, all_rung)

    pieces = whole_radial_pieces(all_embedding, squares, inverse_scale)
    solution = jnp.zeros_like(all_targets)
    residual = all_targets
    direction = all_targets
    gram = outer_gram(residual, residual)
    for iteration in range(ITERS):
        image = (
            kernel_image(
                all_embedding, squares, rung_onehot, col_fidelity, inverse_scale, direction,
                pieces,
            )
            + noise_var[0] * direction
        )
        curvature = outer_gram(direction, image)
        step_matrix = solve_spd(curvature, gram)
        if iteration + 1 == ITERS:
            own = lambda values: lax.dynamic_slice_in_dim(values, own_first, own_count, 1)
            solution, residual, direction, image = (
                own(solution), own(residual), own(direction), own(image)
            )
        solution = solution + jnp.dot(step_matrix.T, direction, precision=lax.Precision.HIGHEST)
        residual = residual - jnp.dot(step_matrix.T, image, precision=lax.Precision.HIGHEST)
        if iteration + 1 < ITERS:
            new_gram = outer_gram(residual, residual)
            update_matrix = solve_spd(gram, new_gram)
            direction = residual + jnp.dot(
                update_matrix.T, direction, precision=lax.Precision.HIGHEST
            )
            gram = new_gram
    return (solution, residual)


def solution(mesh):
    placed = (
        P(None, ("task", "row", "col")),
        P(("task", "row", "col")),
        P(),
        P(),
        P(),
        P(),
        P(),
        P(None, ("task", "row", "col")),
        P("task", None),
        P("task"),
        P("task"),
    )
    return jax.shard_map(
        on_device,
        mesh=mesh,
        in_specs=placed,
        out_specs=(P(None, ("task", "row", "col")), P(None, ("task", "row", "col"))),
        check_vma=False,
    )
```
